256 devices in a mesh: tm: 16 (over z, core), head: 16 (over y, x).
Axes of the slice: x: 4, y: 4, z: 8, core: 2. Of those that a mesh axis runs over, the one named last changes fastest.
Arguments:
- frames: bfloat16 [8192, 2048], P(('tm', 'head')), may hold values from -6 to 6
- log_decay: float32 [8192, 16], P('tm', 'head'), may hold values from -2 to 0, as said below
- w_query: bfloat16 [2048, 2048], P('tm', 'head'), may hold values from -0.125 to 0.125
- w_key: bfloat16 [2048, 2048], P('tm', 'head'), may hold values from -0.125 to 0.125
- w_value: bfloat16 [2048, 2048], P('tm', 'head'), may hold values from -0.125 to 0.125
- w_gate: bfloat16 [2048, 2048], P('tm', 'head'), may hold values from -0.125 to 0.125
- w_out: bfloat16 [2048, 2048], P('head', 'tm'), may hold values from -0.125 to 0.125
Outputs:
- mixed: bfloat16 [8192, 2048], P(('tm', 'head'))
The draws below stay inside these ranges and needn't reach their ends.
Inputs may be any that keep to these rules, and one draw needn't show every extreme that they name: `log_decay`: strictly negative.
All inputs are finite; a program needn't handle non-finite values.
Results may differ from the reference program's by a relative error of at most 0.015.
Values may be sent and summed in bfloat16 or wider, within the bound.
No kernel may reach another device: no remote copies, remote signals or barrier semaphores. Data moves between devices by JAX's collectives and lax.ppermute only.
A program may use at most 64 MiB of HBM per device.

```python
import jax
import jax.numpy as jnp
from jax import lax

MEMORY_GROUPS = 16
HEAD_DIM = 128
D = 2048
BLOCK = 512
TOK_DEV = 512
AUDIO_SLICES = 8192


def draw_log_decay(key, part):
    noise_seed_collection = jax.random.split(key, 7)
    quick_share = 0.5
    quick_heads = jax.random.uniform(noise_seed_collection[0], (MEMORY_GROUPS,)) < quick_share
    slow_rate = 2.302585 / AUDIO_SLICES * jax.random.uniform(noise_seed_collection[1], (MEMORY_GROUPS,), minval=0.1, maxval=0.25)
    quick_rate = 1.0 / jax.random.uniform(noise_seed_collection[2], (MEMORY_GROUPS,), minval=30.0, maxval=50.0)
    floor_decay_speed = jnp.where(quick_heads, quick_rate, slow_rate)
    span_count = AUDIO_SLICES // TOK_DEV
    width_factor = jnp.exp(jax.random.uniform(noise_seed_collection[3], (span_count, MEMORY_GROUPS), minval=-0.693, maxval=0.693))
    width_factor = jnp.repeat(width_factor, TOK_DEV, axis=0)
    noise_jitter = jax.random.uniform(noise_seed_collection[4], (AUDIO_SLICES, MEMORY_GROUPS), minval=0.3, maxval=1.7)
    slices_within_segment = jax.random.randint(noise_seed_collection[5], (2, MEMORY_GROUPS), 0, AUDIO_SLICES)
    segment_damping = jnp.log(jax.random.uniform(noise_seed_collection[6], (2, MEMORY_GROUPS), minval=0.5, maxval=0.8))
    slice_ordinal = jnp.arange(AUDIO_SLICES, dtype=jnp.int32)[:, None]
    segment_collection = jnp.where(slice_ordinal == slices_within_segment[0][None, :], segment_damping[0][None, :], 0.0)
    segment_collection = segment_collection + jnp.where(slice_ordinal == slices_within_segment[1][None, :], segment_damping[1][None, :], 0.0)
    return (-floor_decay_speed[None, :] * width_factor * noise_jitter + segment_collection).astype(jnp.float32)


def levels(rng, shape, pieces, low, top_value):
    level = 1.0
    for axis_at, shards_of in pieces:
        steps = jax.random.uniform(jax.random.fold_in(jax.random.fold_in(rng, 6), axis_at), (shards_of,), jnp.float32, low / len(pieces), top_value / len(pieces))
        level = level * jnp.repeat(jnp.exp(steps), shape[axis_at] // shards_of).reshape((-1,) + (1,) * (len(shape) - 1 - axis_at))
    return level


def noise(stream_key, shape, width, limit, cuts=(), kind=jnp.bfloat16):
    entries = width * jax.random.normal(stream_key, shape, jnp.float32)
    if cuts:
        entries = entries * levels(stream_key, shape, cuts, -0.22, 0.18)
    return jnp.clip(entries, -limit, limit).astype(kind)


def setup_inputs(seed: int = 0) -> dict:
    key_list = jax.random.split(jax.random.key(seed), 8)
    return {
        "frames": noise(key_list[0], (AUDIO_SLICES, D), 1.0, 6.0, ((0, 256),)),
        "log_decay": draw_log_decay(jax.random.fold_in(key_list[7], 71), 0),
        "w_query": noise(key_list[2], (D, D), D ** -0.5, 0.125, ((0, 16), (1, 16))),
        "w_key": noise(key_list[3], (D, D), D ** -0.5, 0.125, ((0, 16), (1, 16))),
        "w_value": noise(key_list[4], (D, D), D ** -0.5, 0.125, ((0, 16), (1, 16))),
        "w_gate": noise(key_list[5], (D, D), D ** -0.5, 0.125, ((0, 16), (1, 16))),
        "w_out": noise(key_list[6], (D, D), D ** -0.5, 0.125, ((0, 16), (1, 16))),
    }


def reference(frames, log_decay, w_query, w_key, w_value, w_gate, w_out):
    query_all = jnp.dot(frames, w_query, preferred_element_type=jnp.float32).astype(jnp.bfloat16)
    key_all = jnp.dot(frames, w_key, preferred_element_type=jnp.float32).astype(jnp.bfloat16)
    value_all = jnp.dot(frames, w_value, preferred_element_type=jnp.float32).astype(jnp.bfloat16)
    gate_all = jnp.dot(frames, w_gate, preferred_element_type=jnp.float32)
    block_count = AUDIO_SLICES // BLOCK
    query_blocks = query_all.reshape(block_count, BLOCK, MEMORY_GROUPS, HEAD_DIM)
    key_blocks = key_all.reshape(block_count, BLOCK, MEMORY_GROUPS, HEAD_DIM)
    value_blocks = value_all.reshape(block_count, BLOCK, MEMORY_GROUPS, HEAD_DIM)
    decay_blocks = log_decay.reshape(block_count, BLOCK, MEMORY_GROUPS)
    slice_ordinal = jnp.arange(BLOCK, dtype=jnp.int32)
    causal = slice_ordinal[:, None] >= slice_ordinal[None, :]

    def advance(carry_state, inputs):
        query_block, key_block, value_block, decay_block = inputs
        running = jnp.cumsum(decay_block, axis=0)
        gaps = running.T[:, :, None] - running.T[:, None, :]
        decay = jnp.exp(jnp.where(causal[None], gaps, -jnp.inf))
        scores = jnp.einsum('thd,shd->hts', query_block.astype(jnp.float32), key_block.astype(jnp.float32))
        weights = (scores * decay).astype(jnp.bfloat16)
        intra = jnp.einsum('hts,shd->thd', weights.astype(jnp.float32), value_block.astype(jnp.float32))
        lifted = query_block.astype(jnp.float32) * jnp.exp(running)[:, :, None]
        inter = jnp.einsum('thd,hde->the', lifted, carry_state, precision=lax.Precision.HIGHEST)
        scaled = (key_block.astype(jnp.float32) * jnp.exp(running[-1][None, :] - running)[:, :, None]).astype(jnp.bfloat16)
        update = jnp.einsum('shd,she->hde', scaled.astype(jnp.float32), value_block.astype(jnp.float32))
        next_state = jnp.exp(running[-1])[:, None, None] * carry_state + update
        return (next_state, intra + inter)
    start_state = jnp.zeros((MEMORY_GROUPS, HEAD_DIM, HEAD_DIM), jnp.float32)
    _, retained = lax.scan(advance, start_state, (query_blocks, key_blocks, value_blocks, decay_blocks))
    retained = retained.reshape(AUDIO_SLICES, MEMORY_GROUPS, HEAD_DIM)
    center = lax.optimization_barrier(jnp.mean(retained, axis=-1, keepdims=True))
    spread = lax.optimization_barrier(jnp.mean((retained - center) ** 2, axis=-1, keepdims=True))
    normed = (retained - center) / jnp.sqrt(spread + 1e-05)
    gated = (jax.nn.silu(gate_all.reshape(AUDIO_SLICES, MEMORY_GROUPS, HEAD_DIM)) * normed).astype(jnp.bfloat16).reshape(AUDIO_SLICES, D)
    return jnp.dot(gated, w_out, preferred_element_type=jnp.float32).astype(jnp.bfloat16)
```

```python
import jax
import jax.numpy as jnp
from jax import lax
from jax.sharding import PartitionSpec as P

HEAD_DIM = 128
BLOCK = 512
PAD_ROWS = 8


def prior_state(local_final, log_total, axis):
    heads_here = local_final.shape[0]
    extra = jnp.broadcast_to(log_total[:, None, None], (heads_here, PAD_ROWS, HEAD_DIM))
    packed = jnp.concatenate([local_final, extra], axis=1)
    gathered = lax.all_gather(packed, axis)
    finals = gathered[:, :, :HEAD_DIM, :]
    totals = gathered[:, :, HEAD_DIM, 0]
    count = gathered.shape[0]
    mine = lax.axis_index(axis)
    order = jnp.arange(count, dtype=jnp.int32)
    between = (order[:, None] < order[None, :]) & (order[None, :] < mine)
    exponent = jnp.sum(jnp.where(between[:, :, None], totals[None, :, :], 0.0), axis=1)
    weight = jnp.where((order < mine)[:, None], jnp.exp(exponent), 0.0)
    return jnp.sum(weight[:, :, None, None] * finals, axis=0)


def shards(frames, log_decay, w_query, w_key, w_value, w_gate, w_out):
    head_width = w_query.shape[1]
    joined = lax.all_gather(
        jnp.concatenate([w_query, w_key, w_value, w_gate], axis=1), "tm", axis=0, tiled=True
    )
    projected = jnp.dot(
        lax.all_gather(frames, "head", axis=0, tiled=True),
        joined,
        preferred_element_type=jnp.float32,
    )
    local_len = projected.shape[0]
    heads_here = head_width // HEAD_DIM
    block_count = local_len // BLOCK
    query_blocks = (
        projected[:, :head_width]
        .astype(jnp.bfloat16)
        .reshape(block_count, BLOCK, heads_here, HEAD_DIM)
    )
    key_blocks = (
        projected[:, head_width : 2 * head_width]
        .astype(jnp.bfloat16)
        .reshape(block_count, BLOCK, heads_here, HEAD_DIM)
    )
    value_blocks = (
        projected[:, 2 * head_width : 3 * head_width]
        .astype(jnp.bfloat16)
        .reshape(block_count, BLOCK, heads_here, HEAD_DIM)
    )
    gate_all = projected[:, 3 * head_width :]
    running_blocks = jnp.cumsum(log_decay.reshape(block_count, BLOCK, heads_here), axis=1)
    slice_ordinal = jnp.arange(BLOCK, dtype=jnp.int32)
    causal = slice_ordinal[:, None] >= slice_ordinal[None, :]

    def local_step(carry_state, inputs):
        query_block, key_block, value_block, running = inputs
        gaps = running.T[:, :, None] - running.T[:, None, :]
        decay = jnp.exp(jnp.where(causal[None], gaps, -jnp.inf))
        scores = jnp.einsum(
            "thd,shd->hts", query_block, key_block, preferred_element_type=jnp.float32
        )
        weights = (scores * decay).astype(jnp.bfloat16)
        intra = jnp.einsum("hts,shd->thd", weights, value_block, preferred_element_type=jnp.float32)
        scaled = (
            key_block.astype(jnp.float32) * jnp.exp(running[-1][None, :] - running)[:, :, None]
        ).astype(jnp.bfloat16)
        update = jnp.einsum("shd,she->hde", scaled, value_block, preferred_element_type=jnp.float32)
        next_state = jnp.exp(running[-1])[:, None, None] * carry_state + update
        return (next_state, (intra, carry_state))

    zero_state = jnp.zeros((heads_here, HEAD_DIM, HEAD_DIM), jnp.float32)
    local_final, (intra_all, local_starts) = lax.scan(
        local_step, zero_state, (query_blocks, key_blocks, value_blocks, running_blocks)
    )
    prior = prior_state(local_final, jnp.sum(log_decay, axis=0), "tm")
    block_logs = running_blocks[:, -1, :]
    before = jnp.cumsum(block_logs, axis=0) - block_logs
    start_states = jnp.exp(before)[:, :, None, None] * prior[None] + local_starts
    lifted = query_blocks.astype(jnp.float32) * jnp.exp(running_blocks)[..., None]
    inter = jnp.einsum("cthd,chde->cthe", lifted, start_states, precision=lax.Precision.HIGHEST)
    retained = (intra_all + inter).reshape(local_len, heads_here, HEAD_DIM)
    center = jnp.mean(retained, axis=-1, keepdims=True)
    spread = jnp.mean((retained - center) ** 2, axis=-1, keepdims=True)
    normed = (retained - center) / jnp.sqrt(spread + 1e-05)
    gated = (
        (jax.nn.silu(gate_all.reshape(local_len, heads_here, HEAD_DIM)) * normed)
        .astype(jnp.bfloat16)
        .reshape(local_len, head_width)
    )
    owned = lax.all_to_all(gated, "head", split_axis=0, concat_axis=1, tiled=True)
    rows_out = lax.all_gather(w_out, "tm", axis=1, tiled=True)
    return jnp.dot(
        owned,
        lax.all_gather(rows_out, "head", axis=0, tiled=True),
        preferred_element_type=jnp.float32,
    ).astype(jnp.bfloat16)


def solution(mesh):
    return jax.shard_map(
        shards,
        mesh=mesh,
        in_specs=(
            P(("tm", "head"), None),
            P("tm", "head"),
            P("tm", "head"),
            P("tm", "head"),
            P("tm", "head"),
            P("tm", "head"),
            P("head", "tm"),
        ),
        out_specs=P(("tm", "head"), None),
        check_vma=False,
    )
```

```python
import jax
import jax.numpy as jnp
from jax import lax
from jax.sharding import PartitionSpec as P

HEAD_DIM = 128
BLOCK = 512
PAD_ROWS = 8


def gather_by_exchange(part, axis):
    count = lax.axis_size(axis)
    copies = jnp.broadcast_to(part[None], (count,) + part.shape)
    return lax.all_to_all(copies, axis, 0, 0, tiled=False)


def prior_state(local_final, log_total, axis):
    heads_here = local_final.shape[0]
    extra = jnp.broadcast_to(log_total[:, None, None], (heads_here, PAD_ROWS, HEAD_DIM))
    packed = jnp.concatenate([local_final, extra], axis=1)
    gathered = gather_by_exchange(packed, axis)
    finals = gathered[:, :, :HEAD_DIM, :]
    totals = gathered[:, :, HEAD_DIM, 0]
    count = gathered.shape[0]
    mine = lax.axis_index(axis)
    order = jnp.arange(count, dtype=jnp.int32)
    between = (order[:, None] < order[None, :]) & (order[None, :] < mine)
    exponent = jnp.sum(jnp.where(between[:, :, None], totals[None, :, :], 0.0), axis=1)
    weight = jnp.where((order < mine)[:, None], jnp.exp(exponent), 0.0)
    return jnp.sum(weight[:, :, None, None] * finals, axis=0)


def shards(frames, log_decay, w_query, w_key, w_value, w_gate, w_out):
    head_width = w_query.shape[1]
    joined = lax.all_gather(
        jnp.concatenate([w_query, w_key, w_value, w_gate], axis=1), "tm", axis=0, tiled=True
    )
    rows_out = lax.all_gather(w_out, "tm", axis=1, tiled=True)
    frames_here = gather_by_exchange(frames, "head").reshape(-1, frames.shape[1])
    projected = jnp.dot(
        frames_here,
        joined,
        preferred_element_type=jnp.float32,
    )
    local_len = projected.shape[0]
    heads_here = head_width // HEAD_DIM
    block_count = local_len // BLOCK
    query_blocks = (
        projected[:, :head_width]
        .astype(jnp.bfloat16)
        .reshape(block_count, BLOCK, heads_here, HEAD_DIM)
    )
    key_blocks = (
        projected[:, head_width : 2 * head_width]
        .astype(jnp.bfloat16)
        .reshape(block_count, BLOCK, heads_here, HEAD_DIM)
    )
    value_blocks = (
        projected[:, 2 * head_width : 3 * head_width]
        .astype(jnp.bfloat16)
        .reshape(block_count, BLOCK, heads_here, HEAD_DIM)
    )
    gate_all = projected[:, 3 * head_width :]
    running_blocks = jnp.cumsum(log_decay.reshape(block_count, BLOCK, heads_here), axis=1)
    slice_ordinal = jnp.arange(BLOCK, dtype=jnp.int32)
    causal = slice_ordinal[:, None] >= slice_ordinal[None, :]

    def local_step(carry_state, inputs):
        query_block, key_block, value_block, running = inputs
        gaps = running.T[:, :, None] - running.T[:, None, :]
        decay = jnp.exp(jnp.where(causal[None], gaps, -jnp.inf))
        scores = jnp.einsum(
            "thd,shd->hts", query_block, key_block, preferred_element_type=jnp.float32
        )
        weights = (scores * decay).astype(jnp.bfloat16)
        intra = jnp.einsum("hts,shd->thd", weights, value_block, preferred_element_type=jnp.float32)
        scaled = (
            key_block.astype(jnp.float32) * jnp.exp(running[-1][None, :] - running)[:, :, None]
        ).astype(jnp.bfloat16)
        update = jnp.einsum("shd,she->hde", scaled, value_block, preferred_element_type=jnp.float32)
        next_state = jnp.exp(running[-1])[:, None, None] * carry_state + update
        return (next_state, (intra, carry_state))

    zero_state = jnp.zeros((heads_here, HEAD_DIM, HEAD_DIM), jnp.float32)
    local_final, (intra_all, local_starts) = lax.scan(
        local_step, zero_state, (query_blocks, key_blocks, value_blocks, running_blocks)
    )
    prior = prior_state(local_final, jnp.sum(log_decay, axis=0), "tm")
    block_logs = running_blocks[:, -1, :]
    before = jnp.cumsum(block_logs, axis=0) - block_logs
    start_states = jnp.exp(before)[:, :, None, None] * prior[None] + local_starts
    lifted = query_blocks.astype(jnp.float32) * jnp.exp(running_blocks)[..., None]
    inter = jnp.einsum("cthd,chde->cthe", lifted, start_states, precision=lax.Precision.HIGHEST)
    retained = (intra_all + inter).reshape(local_len, heads_here, HEAD_DIM)
    center = jnp.mean(retained, axis=-1, keepdims=True)
    spread = jnp.mean((retained - center) ** 2, axis=-1, keepdims=True)
    normed = (retained - center) / jnp.sqrt(spread + 1e-05)
    gated = (
        (jax.nn.silu(gate_all.reshape(local_len, heads_here, HEAD_DIM)) * normed)
        .astype(jnp.bfloat16)
        .reshape(local_len, head_width)
    )
    share = jnp.dot(gated, rows_out, preferred_element_type=jnp.float32).astype(jnp.bfloat16)
    owners = lax.axis_size("head")
    shares = lax.all_to_all(
        share.reshape(owners, local_len // owners, share.shape[1]), "head", 0, 0, tiled=False
    )
    return jnp.sum(shares.astype(jnp.float32), axis=0).astype(jnp.bfloat16)


def solution(mesh):
    return jax.shard_map(
        shards,
        mesh=mesh,
        in_specs=(
            P(("tm", "head"), None),
            P("tm", "head"),
            P("tm", "head"),
            P("tm", "head"),
            P("tm", "head"),
            P("tm", "head"),
            P("head", "tm"),
        ),
        out_specs=P(("tm", "head"), None),
        check_vma=False,
    )
```

```python
import jax
import jax.numpy as jnp
from jax import lax
from jax.sharding import PartitionSpec as P

HEAD_DIM = 128
BLOCK = 512
PAD_ROWS = 8


def gather_by_exchange(part, axis):
    count = lax.axis_size(axis)
    copies = jnp.broadcast_to(part[None], (count,) + part.shape)
    return lax.all_to_all(copies, axis, 0, 0, tiled=False)


def prior_state(local_final, log_total, axis):
    heads_here = local_final.shape[0]
    extra = jnp.broadcast_to(log_total[:, None, None], (heads_here, PAD_ROWS, HEAD_DIM))
    packed = jnp.concatenate([local_final, extra], axis=1)
    gathered = gather_by_exchange(packed, axis)
    finals = gathered[:, :, :HEAD_DIM, :]
    totals = gathered[:, :, HEAD_DIM, 0]
    count = gathered.shape[0]
    mine = lax.axis_index(axis)
    order = jnp.arange(count, dtype=jnp.int32)
    between = (order[:, None] < order[None, :]) & (order[None, :] < mine)
    exponent = jnp.sum(jnp.where(between[:, :, None], totals[None, :, :], 0.0), axis=1)
    weight = jnp.where((order < mine)[:, None], jnp.exp(exponent), 0.0)
    return jnp.sum(weight[:, :, None, None] * finals, axis=0)


def shards(frames, log_decay, w_query, w_key, w_value, w_gate, w_out):
    head_width = w_query.shape[1]
    stacked = lax.all_gather(
        jnp.concatenate([w_query, w_key, w_value, w_gate, w_out], axis=1), "tm", axis=0, tiled=True
    )
    joined = stacked[:, : 4 * head_width]
    out_blocks = stacked[:, 4 * head_width :].reshape(-1, head_width, w_out.shape[1])
    frames_here = gather_by_exchange(frames, "head").reshape(-1, frames.shape[1])
    projected = jnp.dot(
        frames_here,
        joined,
        preferred_element_type=jnp.float32,
    )
    local_len = projected.shape[0]
    heads_here = head_width // HEAD_DIM
    block_count = local_len // BLOCK
    query_blocks = (
        projected[:, :head_width]
        .astype(jnp.bfloat16)
        .reshape(block_count, BLOCK, heads_here, HEAD_DIM)
    )
    key_blocks = (
        projected[:, head_width : 2 * head_width]
        .astype(jnp.bfloat16)
        .reshape(block_count, BLOCK, heads_here, HEAD_DIM)
    )
    value_blocks = (
        projected[:, 2 * head_width : 3 * head_width]
        .astype(jnp.bfloat16)
        .reshape(block_count, BLOCK, heads_here, HEAD_DIM)
    )
    gate_all = projected[:, 3 * head_width :]
    running_blocks = jnp.cumsum(log_decay.reshape(block_count, BLOCK, heads_here), axis=1)
    slice_ordinal = jnp.arange(BLOCK, dtype=jnp.int32)
    causal = slice_ordinal[:, None] >= slice_ordinal[None, :]

    def local_step(carry_state, inputs):
        query_block, key_block, value_block, running = inputs
        gaps = running.T[:, :, None] - running.T[:, None, :]
        decay = jnp.exp(jnp.where(causal[None], gaps, -jnp.inf))
        scores = jnp.einsum(
            "thd,shd->hts", query_block, key_block, preferred_element_type=jnp.float32
        )
        weights = (scores * decay).astype(jnp.bfloat16)
        intra = jnp.einsum("hts,shd->thd", weights, value_block, preferred_element_type=jnp.float32)
        scaled = (
            key_block.astype(jnp.float32) * jnp.exp(running[-1][None, :] - running)[:, :, None]
        ).astype(jnp.bfloat16)
        update = jnp.einsum("shd,she->hde", scaled, value_block, preferred_element_type=jnp.float32)
        next_state = jnp.exp(running[-1])[:, None, None] * carry_state + update
        return (next_state, (intra, carry_state))

    zero_state = jnp.zeros((heads_here, HEAD_DIM, HEAD_DIM), jnp.float32)
    local_final, (intra_all, local_starts) = lax.scan(
        local_step, zero_state, (query_blocks, key_blocks, value_blocks, running_blocks)
    )
    prior = prior_state(local_final, jnp.sum(log_decay, axis=0), "tm")
    block_logs = running_blocks[:, -1, :]
    before = jnp.cumsum(block_logs, axis=0) - block_logs
    start_states = jnp.exp(before)[:, :, None, None] * prior[None] + local_starts
    lifted = query_blocks.astype(jnp.float32) * jnp.exp(running_blocks)[..., None]
    inter = jnp.einsum("cthd,chde->cthe", lifted, start_states, precision=lax.Precision.HIGHEST)
    retained = (intra_all + inter).reshape(local_len, heads_here, HEAD_DIM)
    center = jnp.mean(retained, axis=-1, keepdims=True)
    spread = jnp.mean((retained - center) ** 2, axis=-1, keepdims=True)
    normed = (retained - center) / jnp.sqrt(spread + 1e-05)
    gated = (
        (jax.nn.silu(gate_all.reshape(local_len, heads_here, HEAD_DIM)) * normed)
        .astype(jnp.bfloat16)
        .reshape(local_len, head_width)
    )
    share = (
        jnp.einsum("fr,krc->fkc", gated, out_blocks, preferred_element_type=jnp.float32)
        .astype(jnp.bfloat16)
        .reshape(local_len, -1)
    )
    owners = lax.axis_size("head")
    shares = lax.all_to_all(
        share.reshape(owners, local_len // owners, share.shape[1]), "head", 0, 0, tiled=False
    )
    return jnp.sum(shares.astype(jnp.float32), axis=0).astype(jnp.bfloat16)


def solution(mesh):
    return jax.shard_map(
        shards,
        mesh=mesh,
        in_specs=(
            P(("tm", "head"), None),
            P("tm", "head"),
            P("tm", "head"),
            P("tm", "head"),
            P("tm", "head"),
            P("tm", "head"),
            P("head", "tm"),
        ),
        out_specs=P(("tm", "head"), None),
        check_vma=False,
    )
```

```python
import jax
import jax.numpy as jnp
from jax import lax
from jax.sharding import PartitionSpec as P

HEAD_DIM = 128
BLOCK = 512
PAD_ROWS = 8


def gather_by_exchange(part, axis):
    count = lax.axis_size(axis)
    copies = jnp.broadcast_to(part[None], (count,) + part.shape)
    return lax.all_to_all(copies, axis, 0, 0, tiled=False)


def prior_state(local_final, log_total, axis):
    heads_here = local_final.shape[0]
    extra = jnp.broadcast_to(log_total[:, None, None], (heads_here, PAD_ROWS, HEAD_DIM))
    packed = jnp.concatenate([local_final, extra], axis=1)
    gathered = gather_by_exchange(packed, axis)
    finals = gathered[:, :, :HEAD_DIM, :]
    totals = gathered[:, :, HEAD_DIM, 0]
    count = gathered.shape[0]
    mine = lax.axis_index(axis)
    order = jnp.arange(count, dtype=jnp.int32)
    between = (order[:, None] < order[None, :]) & (order[None, :] < mine)
    exponent = jnp.sum(jnp.where(between[:, :, None], totals[None, :, :], 0.0), axis=1)
    weight = jnp.where((order < mine)[:, None], jnp.exp(exponent), 0.0)
    return jnp.sum(weight[:, :, None, None] * finals, axis=0)


def shards(frames, log_decay, w_query, w_key, w_value, w_gate, w_out):
    head_width = w_query.shape[1]
    stacked = lax.all_gather(
        jnp.concatenate([w_query, w_key, w_value, w_gate, w_out], axis=1), "tm", axis=0, tiled=True
    )
    joined = stacked[:, : 4 * head_width]
    out_blocks = stacked[:, 4 * head_width :].reshape(-1, head_width, w_out.shape[1])
    frames_here = gather_by_exchange(frames, "head").reshape(-1, frames.shape[1])
    projected = jnp.dot(
        frames_here,
        joined,
        preferred_element_type=jnp.float32,
    )
    local_len = projected.shape[0]
    heads_here = head_width // HEAD_DIM
    block_count = local_len // BLOCK
    query_blocks = (
        projected[:, :head_width]
        .astype(jnp.bfloat16)
        .reshape(block_count, BLOCK, heads_here, HEAD_DIM)
    )
    key_blocks = (
        projected[:, head_width : 2 * head_width]
        .astype(jnp.bfloat16)
        .reshape(block_count, BLOCK, heads_here, HEAD_DIM)
    )
    value_blocks = (
        projected[:, 2 * head_width : 3 * head_width]
        .astype(jnp.bfloat16)
        .reshape(block_count, BLOCK, heads_here, HEAD_DIM)
    )
    gate_all = projected[:, 3 * head_width :]
    running_blocks = jnp.cumsum(log_decay.reshape(block_count, BLOCK, heads_here), axis=1)
    slice_ordinal = jnp.arange(BLOCK, dtype=jnp.int32)
    causal = slice_ordinal[:, None] >= slice_ordinal[None, :]

    def local_step(carry_state, inputs):
        query_block, key_block, value_block, running = inputs
        gaps = running.T[:, :, None] - running.T[:, None, :]
        decay = jnp.exp(jnp.where(causal[None], gaps, -jnp.inf))
        scores = jnp.einsum(
            "thd,shd->hts", query_block, key_block, preferred_element_type=jnp.float32
        )
        weights = (scores * decay).astype(jnp.bfloat16)
        intra = jnp.einsum("hts,shd->thd", weights, value_block, preferred_element_type=jnp.float32)
        scaled = (
            key_block.astype(jnp.float32) * jnp.exp(running[-1][None, :] - running)[:, :, None]
        ).astype(jnp.bfloat16)
        update = jnp.einsum("shd,she->hde", scaled, value_block, preferred_element_type=jnp.float32)
        next_state = jnp.exp(running[-1])[:, None, None] * carry_state + update
        return (next_state, (intra, carry_state))

    zero_state = jnp.zeros((heads_here, HEAD_DIM, HEAD_DIM), jnp.float32)
    local_final, (intra_all, local_starts) = lax.scan(
        local_step, zero_state, (query_blocks, key_blocks, value_blocks, running_blocks)
    )
    prior = prior_state(local_final, jnp.sum(log_decay, axis=0), "tm")
    block_logs = running_blocks[:, -1, :]
    before = jnp.cumsum(block_logs, axis=0) - block_logs
    start_states = jnp.exp(before)[:, :, None, None] * prior[None] + local_starts
    lifted = query_blocks.astype(jnp.float32) * jnp.exp(running_blocks)[..., None]
    inter = jnp.einsum("cthd,chde->cthe", lifted, start_states, precision=lax.Precision.HIGHEST)
    retained = (intra_all + inter).reshape(local_len, heads_here, HEAD_DIM)
    center = jnp.mean(retained, axis=-1, keepdims=True)
    spread = jnp.mean((retained - center) ** 2, axis=-1, keepdims=True)
    normed = (retained - center) / jnp.sqrt(spread + 1e-05)
    gated = (
        (jax.nn.silu(gate_all.reshape(local_len, heads_here, HEAD_DIM)) * normed)
        .astype(jnp.bfloat16)
        .reshape(local_len, head_width)
    )
    heads = lax.axis_size("head")
    side = int(round(heads ** 0.5))
    me = lax.axis_index("head")
    row, col = me // side, me % side
    rows_mine = out_blocks
    by_owner = gated.reshape(side, side, local_len // heads, head_width)
    pieces = [lax.dynamic_index_in_dim(by_owner, col, axis=1, keepdims=False)]
    weights_in = [rows_mine]
    for shift in range(1, side):
        across = [(h, (h // side) * side + (h % side + shift) % side) for h in range(heads)]
        piece = lax.dynamic_index_in_dim(by_owner, (col + shift) % side, axis=1, keepdims=False)
        pieces.append(lax.ppermute(piece, "head", across))
        weights_in.append(lax.ppermute(rows_mine, "head", across))
    partial = jnp.einsum(
        "syfr,skrc->yfkc",
        jnp.stack(pieces),
        jnp.stack(weights_in),
        preferred_element_type=jnp.float32,
    ).astype(jnp.bfloat16)
    partial = partial.reshape(side, local_len // heads, -1)
    total = lax.dynamic_index_in_dim(partial, row, axis=0, keepdims=False).astype(jnp.float32)
    for shift in range(1, side):
        down = [(h, ((h // side + shift) % side) * side + h % side) for h in range(heads)]
        piece = lax.dynamic_index_in_dim(partial, (row + shift) % side, axis=0, keepdims=False)
        total = total + lax.ppermute(piece, "head", down).astype(jnp.float32)
    return total.astype(jnp.bfloat16)


def solution(mesh):
    return jax.shard_map(
        shards,
        mesh=mesh,
        in_specs=(
            P(("tm", "head"), None),
            P("tm", "head"),
            P("tm", "head"),
            P("tm", "head"),
            P("tm", "head"),
            P("tm", "head"),
            P("head", "tm"),
        ),
        out_specs=P(("tm", "head"), None),
        check_vma=False,
    )
```

```python
import jax
import jax.numpy as jnp
from jax import lax
from jax.sharding import PartitionSpec as P

HEAD_DIM = 128
BLOCK = 512
PAD_ROWS = 8


def gather_by_exchange(part, axis):
    count = lax.axis_size(axis)
    copies = jnp.broadcast_to(part[None], (count,) + part.shape)
    return lax.all_to_all(copies, axis, 0, 0, tiled=False)


def prior_state(local_final, log_total, axis):
    heads_here = local_final.shape[0]
    high = log_total.astype(jnp.bfloat16)
    low = (log_total - high.astype(jnp.float32)).astype(jnp.bfloat16)
    extra = jnp.concatenate(
        [
            jnp.broadcast_to(high[:, None, None], (heads_here, 1, HEAD_DIM)),
            jnp.broadcast_to(low[:, None, None], (heads_here, 1, HEAD_DIM)),
            jnp.zeros((heads_here, PAD_ROWS - 2, HEAD_DIM), jnp.bfloat16),
        ],
        axis=1,
    )
    packed = jnp.concatenate([local_final.astype(jnp.bfloat16), extra], axis=1)
    gathered = gather_by_exchange(packed, axis)
    finals = gathered[:, :, :HEAD_DIM, :].astype(jnp.float32)
    totals = gathered[:, :, HEAD_DIM, 0].astype(jnp.float32) + gathered[:, :, HEAD_DIM + 1, 0].astype(
        jnp.float32
    )
    count = gathered.shape[0]
    mine = lax.axis_index(axis)
    order = jnp.arange(count, dtype=jnp.int32)
    between = (order[:, None] < order[None, :]) & (order[None, :] < mine)
    exponent = jnp.sum(jnp.where(between[:, :, None], totals[None, :, :], 0.0), axis=1)
    weight = jnp.where((order < mine)[:, None], jnp.exp(exponent), 0.0)
    return jnp.sum(weight[:, :, None, None] * finals, axis=0)


def shards(frames, log_decay, w_query, w_key, w_value, w_gate, w_out):
    head_width = w_query.shape[1]
    stacked = lax.all_gather(
        jnp.concatenate([w_query, w_key, w_value, w_gate, w_out], axis=1), "tm", axis=0, tiled=True
    )
    joined = stacked[:, : 4 * head_width]
    out_blocks = stacked[:, 4 * head_width :].reshape(-1, head_width, w_out.shape[1])
    frames_here = gather_by_exchange(frames, "head").reshape(-1, frames.shape[1])
    projected = jnp.dot(
        frames_here,
        joined,
        preferred_element_type=jnp.float32,
    )
    local_len = projected.shape[0]
    heads_here = head_width // HEAD_DIM
    block_count = local_len // BLOCK
    query_blocks = (
        projected[:, :head_width]
        .astype(jnp.bfloat16)
        .reshape(block_count, BLOCK, heads_here, HEAD_DIM)
    )
    key_blocks = (
        projected[:, head_width : 2 * head_width]
        .astype(jnp.bfloat16)
        .reshape(block_count, BLOCK, heads_here, HEAD_DIM)
    )
    value_blocks = (
        projected[:, 2 * head_width : 3 * head_width]
        .astype(jnp.bfloat16)
        .reshape(block_count, BLOCK, heads_here, HEAD_DIM)
    )
    gate_all = projected[:, 3 * head_width :]
    running_blocks = jnp.cumsum(log_decay.reshape(block_count, BLOCK, heads_here), axis=1)
    slice_ordinal = jnp.arange(BLOCK, dtype=jnp.int32)
    causal = slice_ordinal[:, None] >= slice_ordinal[None, :]

    def local_step(carry_state, inputs):
        query_block, key_block, value_block, running = inputs
        gaps = running.T[:, :, None] - running.T[:, None, :]
        decay = jnp.exp(jnp.where(causal[None], gaps, -jnp.inf))
        scores = jnp.einsum(
            "thd,shd->hts", query_block, key_block, preferred_element_type=jnp.float32
        )
        weights = (scores * decay).astype(jnp.bfloat16)
        intra = jnp.einsum("hts,shd->thd", weights, value_block, preferred_element_type=jnp.float32)
        scaled = (
            key_block.astype(jnp.float32) * jnp.exp(running[-1][None, :] - running)[:, :, None]
        ).astype(jnp.bfloat16)
        update = jnp.einsum("shd,she->hde", scaled, value_block, preferred_element_type=jnp.float32)
        next_state = jnp.exp(running[-1])[:, None, None] * carry_state + update
        return (next_state, (intra, carry_state))

    zero_state = jnp.zeros((heads_here, HEAD_DIM, HEAD_DIM), jnp.float32)
    local_final, (intra_all, local_starts) = lax.scan(
        local_step, zero_state, (query_blocks, key_blocks, value_blocks, running_blocks)
    )
    prior = prior_state(local_final, jnp.sum(log_decay, axis=0), "tm")
    block_logs = running_blocks[:, -1, :]
    before = jnp.cumsum(block_logs, axis=0) - block_logs
    start_states = jnp.exp(before)[:, :, None, None] * prior[None] + local_starts
    lifted = query_blocks.astype(jnp.float32) * jnp.exp(running_blocks)[..., None]
    inter = jnp.einsum("cthd,chde->cthe", lifted, start_states, precision=lax.Precision.HIGHEST)
    retained = (intra_all + inter).reshape(local_len, heads_here, HEAD_DIM)
    center = jnp.mean(retained, axis=-1, keepdims=True)
    spread = jnp.mean((retained - center) ** 2, axis=-1, keepdims=True)
    normed = (retained - center) / jnp.sqrt(spread + 1e-05)
    gated = (
        (jax.nn.silu(gate_all.reshape(local_len, heads_here, HEAD_DIM)) * normed)
        .astype(jnp.bfloat16)
        .reshape(local_len, head_width)
    )
    heads = lax.axis_size("head")
    side = int(round(heads ** 0.5))
    me = lax.axis_index("head")
    row, col = me // side, me % side
    rows_mine = out_blocks
    by_owner = gated.reshape(side, side, local_len // heads, head_width)
    pieces = [lax.dynamic_index_in_dim(by_owner, col, axis=1, keepdims=False)]
    weights_in = [rows_mine]
    for shift in range(1, side):
        across = [(h, (h // side) * side + (h % side + shift) % side) for h in range(heads)]
        piece = lax.dynamic_index_in_dim(by_owner, (col + shift) % side, axis=1, keepdims=False)
        pieces.append(lax.ppermute(piece, "head", across))
        weights_in.append(lax.ppermute(rows_mine, "head", across))
    partial = jnp.einsum(
        "syfr,skrc->yfkc",
        jnp.stack(pieces),
        jnp.stack(weights_in),
        preferred_element_type=jnp.float32,
    ).astype(jnp.bfloat16)
    partial = partial.reshape(side, local_len // heads, -1)
    total = lax.dynamic_index_in_dim(partial, row, axis=0, keepdims=False).astype(jnp.float32)
    for shift in range(1, side):
        down = [(h, ((h // side + shift) % side) * side + h % side) for h in range(heads)]
        piece = lax.dynamic_index_in_dim(partial, (row + shift) % side, axis=0, keepdims=False)
        total = total + lax.ppermute(piece, "head", down).astype(jnp.float32)
    return total.astype(jnp.bfloat16)


def solution(mesh):
    return jax.shard_map(
        shards,
        mesh=mesh,
        in_specs=(
            P(("tm", "head"), None),
            P("tm", "head"),
            P("tm", "head"),
            P("tm", "head"),
            P("tm", "head"),
            P("tm", "head"),
            P("head", "tm"),
        ),
        out_specs=P(("tm", "head"), None),
        check_vma=False,
    )
```

```python
import jax
import jax.numpy as jnp
from jax import lax
from jax.sharding import PartitionSpec as P

HEAD_DIM = 128
BLOCK = 512
PAD_ROWS = 8


def gather_by_exchange(part, axis):
    count = lax.axis_size(axis)
    copies = jnp.broadcast_to(part[None], (count,) + part.shape)
    return lax.all_to_all(copies, axis, 0, 0, tiled=False)


def prior_state(local_final, log_total, axis):
    heads_here = local_final.shape[0]
    high = log_total.astype(jnp.bfloat16)
    low = (log_total - high.astype(jnp.float32)).astype(jnp.bfloat16)
    extra = jnp.concatenate(
        [
            jnp.broadcast_to(high[:, None, None], (heads_here, 1, HEAD_DIM)),
            jnp.broadcast_to(low[:, None, None], (heads_here, 1, HEAD_DIM)),
            jnp.zeros((heads_here, PAD_ROWS - 2, HEAD_DIM), jnp.bfloat16),
        ],
        axis=1,
    )
    packed = jnp.concatenate([local_final.astype(jnp.bfloat16), extra], axis=1)
    gathered = gather_by_exchange(packed, axis)
    finals = gathered[:, :, :HEAD_DIM, :].astype(jnp.float32)
    totals = gathered[:, :, HEAD_DIM, 0].astype(jnp.float32) + gathered[:, :, HEAD_DIM + 1, 0].astype(
        jnp.float32
    )
    count = gathered.shape[0]
    mine = lax.axis_index(axis)
    order = jnp.arange(count, dtype=jnp.int32)
    between = (order[:, None] < order[None, :]) & (order[None, :] < mine)
    exponent = jnp.sum(jnp.where(between[:, :, None], totals[None, :, :], 0.0), axis=1)
    weight = jnp.where((order < mine)[:, None], jnp.exp(exponent), 0.0)
    return jnp.sum(weight[:, :, None, None] * finals, axis=0)


def shards(frames, log_decay, w_query, w_key, w_value, w_gate, w_out):
    head_width = w_query.shape[1]
    stacked = lax.all_gather(
        jnp.concatenate([w_query, w_key, w_value, w_gate, w_out], axis=1), "tm", axis=0, tiled=True
    )
    joined = stacked[:, : 4 * head_width]
    out_blocks = stacked[:, 4 * head_width :].reshape(-1, head_width, w_out.shape[1])
    frames_here = gather_by_exchange(frames, "head").reshape(-1, frames.shape[1])
    projected = jnp.dot(
        frames_here,
        joined,
        preferred_element_type=jnp.float32,
    )
    local_len = projected.shape[0]
    heads_here = head_width // HEAD_DIM
    block_count = local_len // BLOCK
    query_blocks = (
        projected[:, :head_width]
        .astype(jnp.bfloat16)
        .reshape(block_count, BLOCK, heads_here, HEAD_DIM)
    )
    key_blocks = (
        projected[:, head_width : 2 * head_width]
        .astype(jnp.bfloat16)
        .reshape(block_count, BLOCK, heads_here, HEAD_DIM)
    )
    value_blocks = (
        projected[:, 2 * head_width : 3 * head_width]
        .astype(jnp.bfloat16)
        .reshape(block_count, BLOCK, heads_here, HEAD_DIM)
    )
    gate_all = projected[:, 3 * head_width :]
    running_blocks = jnp.cumsum(log_decay.reshape(block_count, BLOCK, heads_here), axis=1)
    slice_ordinal = jnp.arange(BLOCK, dtype=jnp.int32)
    causal = slice_ordinal[:, None] >= slice_ordinal[None, :]

    def local_step(carry_state, inputs):
        query_block, key_block, value_block, running = inputs
        gaps = running.T[:, :, None] - running.T[:, None, :]
        decay = jnp.exp(jnp.where(causal[None], gaps, -jnp.inf))
        scores = jnp.einsum(
            "thd,shd->hts", query_block, key_block, preferred_element_type=jnp.float32
        )
        weights = (scores * decay).astype(jnp.bfloat16)
        intra = jnp.einsum("hts,shd->thd", weights, value_block, preferred_element_type=jnp.float32)
        scaled = (
            key_block.astype(jnp.float32) * jnp.exp(running[-1][None, :] - running)[:, :, None]
        ).astype(jnp.bfloat16)
        update = jnp.einsum("shd,she->hde", scaled, value_block, preferred_element_type=jnp.float32)
        next_state = jnp.exp(running[-1])[:, None, None] * carry_state + update
        return (next_state, (intra, carry_state))

    zero_state = jnp.zeros((heads_here, HEAD_DIM, HEAD_DIM), jnp.float32)
    local_final, (intra_all, local_starts) = lax.scan(
        local_step, zero_state, (query_blocks, key_blocks, value_blocks, running_blocks)
    )
    prior = prior_state(local_final, jnp.sum(log_decay, axis=0), "tm")
    block_logs = running_blocks[:, -1, :]
    before = jnp.cumsum(block_logs, axis=0) - block_logs
    start_states = jnp.exp(before)[:, :, None, None] * prior[None] + local_starts
    lifted = query_blocks.astype(jnp.float32) * jnp.exp(running_blocks)[..., None]
    inter = jnp.einsum("cthd,chde->cthe", lifted, start_states, precision=lax.Precision.HIGHEST)
    retained = (intra_all + inter).reshape(local_len, heads_here, HEAD_DIM)
    center = jnp.mean(retained, axis=-1, keepdims=True)
    spread = jnp.mean((retained - center) ** 2, axis=-1, keepdims=True)
    normed = (retained - center) / jnp.sqrt(spread + 1e-05)
    gated = (
        (jax.nn.silu(gate_all.reshape(local_len, heads_here, HEAD_DIM)) * normed)
        .astype(jnp.bfloat16)
        .reshape(local_len, head_width)
    )
    heads = lax.axis_size("head")
    side = int(round(heads ** 0.5))
    me = lax.axis_index("head")
    row, col = me // side, me % side
    rows_mine = out_blocks
    by_owner = gated.reshape(side, side, local_len // heads, head_width)
    units = lax.axis_size("tm")
    half = rows_mine.shape[0] // 2
    parity = lax.axis_index("tm") % 2
    own_half = lax.dynamic_slice_in_dim(rows_mine, parity * half, half, axis=0)
    pieces = [lax.dynamic_index_in_dim(by_owner, col, axis=1, keepdims=False)]
    fetched = []
    for shift in range(1, side):
        across = [(h, (h // side) * side + (h % side + shift) % side) for h in range(heads)]
        piece = lax.dynamic_index_in_dim(by_owner, (col + shift) % side, axis=1, keepdims=False)
        pieces.append(lax.ppermute(piece, "head", across))
        fetched.append(lax.ppermute(own_half, "head", across))
    fetched = jnp.stack(fetched)
    swapped = lax.ppermute(fetched, "tm", [(t, t ^ 1) for t in range(units)])
    first = jnp.where(parity == 0, fetched, swapped)
    second = jnp.where(parity == 0, swapped, fetched)
    remote = jnp.concatenate([first, second], axis=1)
    weights_in = [rows_mine] + [remote[s] for s in range(side - 1)]
    partial = jnp.einsum(
        "syfr,skrc->yfkc",
        jnp.stack(pieces),
        jnp.stack(weights_in),
        preferred_element_type=jnp.float32,
    ).astype(jnp.bfloat16)
    partial = partial.reshape(side, local_len // heads, -1)
    total = lax.dynamic_index_in_dim(partial, row, axis=0, keepdims=False).astype(jnp.float32)
    for shift in range(1, side):
        down = [(h, ((h // side + shift) % side) * side + h % side) for h in range(heads)]
        piece = lax.dynamic_index_in_dim(partial, (row + shift) % side, axis=0, keepdims=False)
        total = total + lax.ppermute(piece, "head", down).astype(jnp.float32)
    return total.astype(jnp.bfloat16)


def solution(mesh):
    return jax.shard_map(
        shards,
        mesh=mesh,
        in_specs=(
            P(("tm", "head"), None),
            P("tm", "head"),
            P("tm", "head"),
            P("tm", "head"),
            P("tm", "head"),
            P("tm", "head"),
            P("head", "tm"),
        ),
        out_specs=P(("tm", "head"), None),
        check_vma=False,
    )
```

```python
import jax
import jax.numpy as jnp
from jax import lax
from jax.sharding import PartitionSpec as P

HEAD_DIM = 128
BLOCK = 512
PAD_ROWS = 8


def gather_by_exchange(part, axis):
    count = lax.axis_size(axis)
    copies = jnp.broadcast_to(part[None], (count,) + part.shape)
    return lax.all_to_all(copies, axis, 0, 0, tiled=False)


def pack_state(state, log_total):
    heads_here = state.shape[0]
    high = log_total.astype(jnp.bfloat16)
    low = (log_total - high.astype(jnp.float32)).astype(jnp.bfloat16)
    extra = jnp.concatenate(
        [
            jnp.broadcast_to(high[:, None, None], (heads_here, 1, HEAD_DIM)),
            jnp.broadcast_to(low[:, None, None], (heads_here, 1, HEAD_DIM)),
            jnp.zeros((heads_here, PAD_ROWS - 2, HEAD_DIM), jnp.bfloat16),
        ],
        axis=1,
    )
    return jnp.concatenate([state.astype(jnp.bfloat16), extra], axis=1)


def unpack_state(packed):
    state = packed[..., :HEAD_DIM, :].astype(jnp.float32)
    total = packed[..., HEAD_DIM, 0].astype(jnp.float32) + packed[..., HEAD_DIM + 1, 0].astype(
        jnp.float32
    )
    return state, total


def prior_state(local_final, log_total, axis):
    units = lax.axis_size(axis)
    chips = units // 2
    mine = lax.axis_index(axis)
    parity = mine % 2
    chip = mine // 2
    partner_state, partner_total = unpack_state(
        lax.ppermute(pack_state(local_final, log_total), axis, [(t, t ^ 1) for t in range(units)])
    )
    first_state = jnp.where(parity == 0, local_final, partner_state)
    first_total = jnp.where(parity == 0, log_total, partner_total)
    second_state = jnp.where(parity == 0, partner_state, local_final)
    second_total = jnp.where(parity == 0, partner_total, log_total)
    chip_state = jnp.exp(second_total)[:, None, None] * first_state + second_state
    chip_total = first_total + second_total
    chip_packed = pack_state(chip_state, chip_total)
    received = []
    for shift in range(1, chips):
        later = [(2 * z + c, 2 * (z + shift) + c) for z in range(chips - shift) for c in range(2)]
        received.append(lax.ppermute(chip_packed, axis, later))
    states, totals = unpack_state(jnp.stack(received))
    shifts = jnp.arange(1, chips, dtype=jnp.int32)
    exponent = jnp.cumsum(totals, axis=0) - totals
    weight = jnp.where((shifts <= chip)[:, None], jnp.exp(exponent), 0.0)
    entering = jnp.sum(weight[:, :, None, None] * states, axis=0)
    own_first = jnp.exp(first_total)[:, None, None] * entering + first_state
    return jnp.where(parity == 0, entering, own_first)


def shards(frames, log_decay, w_query, w_key, w_value, w_gate, w_out):
    head_width = w_query.shape[1]
    stacked = lax.all_gather(
        jnp.concatenate([w_query, w_key, w_value, w_gate, w_out], axis=1), "tm", axis=0, tiled=True
    )
    joined = stacked[:, : 4 * head_width]
    out_blocks = stacked[:, 4 * head_width :].reshape(-1, head_width, w_out.shape[1])
    frames_here = gather_by_exchange(frames, "head").reshape(-1, frames.shape[1])
    projected = jnp.dot(
        frames_here,
        joined,
        preferred_element_type=jnp.float32,
    )
    local_len = projected.shape[0]
    heads_here = head_width // HEAD_DIM
    block_count = local_len // BLOCK
    query_blocks = (
        projected[:, :head_width]
        .astype(jnp.bfloat16)
        .reshape(block_count, BLOCK, heads_here, HEAD_DIM)
    )
    key_blocks = (
        projected[:, head_width : 2 * head_width]
        .astype(jnp.bfloat16)
        .reshape(block_count, BLOCK, heads_here, HEAD_DIM)
    )
    value_blocks = (
        projected[:, 2 * head_width : 3 * head_width]
        .astype(jnp.bfloat16)
        .reshape(block_count, BLOCK, heads_here, HEAD_DIM)
    )
    gate_all = projected[:, 3 * head_width :]
    running_blocks = jnp.cumsum(log_decay.reshape(block_count, BLOCK, heads_here), axis=1)
    slice_ordinal = jnp.arange(BLOCK, dtype=jnp.int32)
    causal = slice_ordinal[:, None] >= slice_ordinal[None, :]

    def local_step(carry_state, inputs):
        query_block, key_block, value_block, running = inputs
        gaps = running.T[:, :, None] - running.T[:, None, :]
        decay = jnp.exp(jnp.where(causal[None], gaps, -jnp.inf))
        scores = jnp.einsum(
            "thd,shd->hts", query_block, key_block, preferred_element_type=jnp.float32
        )
        weights = (scores * decay).astype(jnp.bfloat16)
        intra = jnp.einsum("hts,shd->thd", weights, value_block, preferred_element_type=jnp.float32)
        scaled = (
            key_block.astype(jnp.float32) * jnp.exp(running[-1][None, :] - running)[:, :, None]
        ).astype(jnp.bfloat16)
        update = jnp.einsum("shd,she->hde", scaled, value_block, preferred_element_type=jnp.float32)
        next_state = jnp.exp(running[-1])[:, None, None] * carry_state + update
        return (next_state, (intra, carry_state))

    zero_state = jnp.zeros((heads_here, HEAD_DIM, HEAD_DIM), jnp.float32)
    local_final, (intra_all, local_starts) = lax.scan(
        local_step, zero_state, (query_blocks, key_blocks, value_blocks, running_blocks)
    )
    prior = prior_state(local_final, jnp.sum(log_decay, axis=0), "tm")
    block_logs = running_blocks[:, -1, :]
    before = jnp.cumsum(block_logs, axis=0) - block_logs
    start_states = jnp.exp(before)[:, :, None, None] * prior[None] + local_starts
    lifted = query_blocks.astype(jnp.float32) * jnp.exp(running_blocks)[..., None]
    inter = jnp.einsum("cthd,chde->cthe", lifted, start_states, precision=lax.Precision.HIGHEST)
    retained = (intra_all + inter).reshape(local_len, heads_here, HEAD_DIM)
    center = jnp.mean(retained, axis=-1, keepdims=True)
    spread = jnp.mean((retained - center) ** 2, axis=-1, keepdims=True)
    normed = (retained - center) / jnp.sqrt(spread + 1e-05)
    gated = (
        (jax.nn.silu(gate_all.reshape(local_len, heads_here, HEAD_DIM)) * normed)
        .astype(jnp.bfloat16)
        .reshape(local_len, head_width)
    )
    heads = lax.axis_size("head")
    side = int(round(heads ** 0.5))
    me = lax.axis_index("head")
    row, col = me // side, me % side
    rows_mine = out_blocks
    by_owner = gated.reshape(side, side, local_len // heads, head_width)
    units = lax.axis_size("tm")
    half = rows_mine.shape[0] // 2
    parity = lax.axis_index("tm") % 2
    own_half = lax.dynamic_slice_in_dim(rows_mine, parity * half, half, axis=0)
    pieces = [lax.dynamic_index_in_dim(by_owner, col, axis=1, keepdims=False)]
    fetched = []
    for shift in range(1, side):
        across = [(h, (h // side) * side + (h % side + shift) % side) for h in range(heads)]
        piece = lax.dynamic_index_in_dim(by_owner, (col + shift) % side, axis=1, keepdims=False)
        pieces.append(lax.ppermute(piece, "head", across))
        fetched.append(lax.ppermute(own_half, "head", across))
    fetched = jnp.stack(fetched)
    swapped = lax.ppermute(fetched, "tm", [(t, t ^ 1) for t in range(units)])
    first = jnp.where(parity == 0, fetched, swapped)
    second = jnp.where(parity == 0, swapped, fetched)
    remote = jnp.concatenate([first, second], axis=1)
    weights_in = [rows_mine] + [remote[s] for s in range(side - 1)]
    partial = jnp.einsum(
        "syfr,skrc->yfkc",
        jnp.stack(pieces),
        jnp.stack(weights_in),
        preferred_element_type=jnp.float32,
    ).astype(jnp.bfloat16)
    partial = partial.reshape(side, local_len // heads, -1)
    total = lax.dynamic_index_in_dim(partial, row, axis=0, keepdims=False).astype(jnp.float32)
    for shift in range(1, side):
        down = [(h, ((h // side + shift) % side) * side + h % side) for h in range(heads)]
        piece = lax.dynamic_index_in_dim(partial, (row + shift) % side, axis=0, keepdims=False)
        total = total + lax.ppermute(piece, "head", down).astype(jnp.float32)
    return total.astype(jnp.bfloat16)


def solution(mesh):
    return jax.shard_map(
        shards,
        mesh=mesh,
        in_specs=(
            P(("tm", "head"), None),
            P("tm", "head"),
            P("tm", "head"),
            P("tm", "head"),
            P("tm", "head"),
            P("tm", "head"),
            P("head", "tm"),
        ),
        out_specs=P(("tm", "head"), None),
        check_vma=False,
    )
```

```python
import jax
import jax.numpy as jnp
from jax import lax
from jax.sharding import PartitionSpec as P

HEAD_DIM = 128
BLOCK = 512
PAD_ROWS = 8


def gather_by_exchange(part, axis):
    count = lax.axis_size(axis)
    copies = jnp.broadcast_to(part[None], (count,) + part.shape)
    return lax.all_to_all(copies, axis, 0, 0, tiled=False)


def prior_state(local_final, log_total, axis):
    heads_here = local_final.shape[0]
    high = log_total.astype(jnp.bfloat16)
    low = (log_total - high.astype(jnp.float32)).astype(jnp.bfloat16)
    extra = jnp.concatenate(
        [
            jnp.broadcast_to(high[:, None, None], (heads_here, 1, HEAD_DIM)),
            jnp.broadcast_to(low[:, None, None], (heads_here, 1, HEAD_DIM)),
            jnp.zeros((heads_here, PAD_ROWS - 2, HEAD_DIM), jnp.bfloat16),
        ],
        axis=1,
    )
    packed = jnp.concatenate([local_final.astype(jnp.bfloat16), extra], axis=1)
    gathered = gather_by_exchange(packed, axis)
    finals = gathered[:, :, :HEAD_DIM, :].astype(jnp.float32)
    totals = gathered[:, :, HEAD_DIM, 0].astype(jnp.float32) + gathered[:, :, HEAD_DIM + 1, 0].astype(
        jnp.float32
    )
    count = gathered.shape[0]
    mine = lax.axis_index(axis)
    order = jnp.arange(count, dtype=jnp.int32)
    between = (order[:, None] < order[None, :]) & (order[None, :] < mine)
    exponent = jnp.sum(jnp.where(between[:, :, None], totals[None, :, :], 0.0), axis=1)
    weight = jnp.where((order < mine)[:, None], jnp.exp(exponent), 0.0)
    return jnp.sum(weight[:, :, None, None] * finals, axis=0)


def shards(frames, log_decay, w_query, w_key, w_value, w_gate, w_out):
    head_width = w_query.shape[1]
    packed = jnp.concatenate([w_query, w_key, w_value, w_gate, w_out], axis=1)
    units = lax.axis_size("tm")
    parity = lax.axis_index("tm") % 2
    same_place = [[t for t in range(units) if t % 2 == p] for p in range(2)]
    mine = lax.all_gather(packed, "tm", axis_index_groups=same_place)
    theirs = lax.ppermute(mine, "tm", [(t, t ^ 1) for t in range(units)])
    by_place = jnp.stack(
        [jnp.where(parity == 0, mine, theirs), jnp.where(parity == 0, theirs, mine)], axis=1
    )
    stacked = by_place.reshape(-1, packed.shape[1])
    joined = stacked[:, : 4 * head_width]
    out_blocks = stacked[:, 4 * head_width :].reshape(-1, head_width, w_out.shape[1])
    frames_here = gather_by_exchange(frames, "head").reshape(-1, frames.shape[1])
    projected = jnp.dot(
        frames_here,
        joined,
        preferred_element_type=jnp.float32,
    )
    local_len = projected.shape[0]
    heads_here = head_width // HEAD_DIM
    block_count = local_len // BLOCK
    query_blocks = (
        projected[:, :head_width]
        .astype(jnp.bfloat16)
        .reshape(block_count, BLOCK, heads_here, HEAD_DIM)
    )
    key_blocks = (
        projected[:, head_width : 2 * head_width]
        .astype(jnp.bfloat16)
        .reshape(block_count, BLOCK, heads_here, HEAD_DIM)
    )
    value_blocks = (
        projected[:, 2 * head_width : 3 * head_width]
        .astype(jnp.bfloat16)
        .reshape(block_count, BLOCK, heads_here, HEAD_DIM)
    )
    gate_all = projected[:, 3 * head_width :]
    running_blocks = jnp.cumsum(log_decay.reshape(block_count, BLOCK, heads_here), axis=1)
    slice_ordinal = jnp.arange(BLOCK, dtype=jnp.int32)
    causal = slice_ordinal[:, None] >= slice_ordinal[None, :]

    def local_step(carry_state, inputs):
        query_block, key_block, value_block, running = inputs
        gaps = running.T[:, :, None] - running.T[:, None, :]
        decay = jnp.exp(jnp.where(causal[None], gaps, -jnp.inf))
        scores = jnp.einsum(
            "thd,shd->hts", query_block, key_block, preferred_element_type=jnp.float32
        )
        weights = (scores * decay).astype(jnp.bfloat16)
        intra = jnp.einsum("hts,shd->thd", weights, value_block, preferred_element_type=jnp.float32)
        scaled = (
            key_block.astype(jnp.float32) * jnp.exp(running[-1][None, :] - running)[:, :, None]
        ).astype(jnp.bfloat16)
        update = jnp.einsum("shd,she->hde", scaled, value_block, preferred_element_type=jnp.float32)
        next_state = jnp.exp(running[-1])[:, None, None] * carry_state + update
        return (next_state, (intra, carry_state))

    zero_state = jnp.zeros((heads_here, HEAD_DIM, HEAD_DIM), jnp.float32)
    local_final, (intra_all, local_starts) = lax.scan(
        local_step, zero_state, (query_blocks, key_blocks, value_blocks, running_blocks)
    )
    prior = prior_state(local_final, jnp.sum(log_decay, axis=0), "tm")
    block_logs = running_blocks[:, -1, :]
    before = jnp.cumsum(block_logs, axis=0) - block_logs
    start_states = jnp.exp(before)[:, :, None, None] * prior[None] + local_starts
    lifted = query_blocks.astype(jnp.float32) * jnp.exp(running_blocks)[..., None]
    inter = jnp.einsum("cthd,chde->cthe", lifted, start_states, precision=lax.Precision.HIGHEST)
    retained = (intra_all + inter).reshape(local_len, heads_here, HEAD_DIM)
    center = jnp.mean(retained, axis=-1, keepdims=True)
    spread = jnp.mean((retained - center) ** 2, axis=-1, keepdims=True)
    normed = (retained - center) / jnp.sqrt(spread + 1e-05)
    gated = (
        (jax.nn.silu(gate_all.reshape(local_len, heads_here, HEAD_DIM)) * normed)
        .astype(jnp.bfloat16)
        .reshape(local_len, head_width)
    )
    heads = lax.axis_size("head")
    side = int(round(heads ** 0.5))
    me = lax.axis_index("head")
    row, col = me // side, me % side
    rows_mine = out_blocks
    by_owner = gated.reshape(side, side, local_len // heads, head_width)
    units = lax.axis_size("tm")
    half = rows_mine.shape[0] // 2
    parity = lax.axis_index("tm") % 2
    own_half = lax.dynamic_slice_in_dim(rows_mine, parity * half, half, axis=0)
    pieces = [lax.dynamic_index_in_dim(by_owner, col, axis=1, keepdims=False)]
    fetched = []
    for shift in range(1, side):
        across = [(h, (h // side) * side + (h % side + shift) % side) for h in range(heads)]
        piece = lax.dynamic_index_in_dim(by_owner, (col + shift) % side, axis=1, keepdims=False)
        pieces.append(lax.ppermute(piece, "head", across))
        fetched.append(lax.ppermute(own_half, "head", across))
    fetched = jnp.stack(fetched)
    swapped = lax.ppermute(fetched, "tm", [(t, t ^ 1) for t in range(units)])
    first = jnp.where(parity == 0, fetched, swapped)
    second = jnp.where(parity == 0, swapped, fetched)
    remote = jnp.concatenate([first, second], axis=1)
    weights_in = [rows_mine] + [remote[s] for s in range(side - 1)]
    partial = jnp.einsum(
        "syfr,skrc->yfkc",
        jnp.stack(pieces),
        jnp.stack(weights_in),
        preferred_element_type=jnp.float32,
    ).astype(jnp.bfloat16)
    partial = partial.reshape(side, local_len // heads, -1)
    total = lax.dynamic_index_in_dim(partial, row, axis=0, keepdims=False).astype(jnp.float32)
    for shift in range(1, side):
        down = [(h, ((h // side + shift) % side) * side + h % side) for h in range(heads)]
        piece = lax.dynamic_index_in_dim(partial, (row + shift) % side, axis=0, keepdims=False)
        total = total + lax.ppermute(piece, "head", down).astype(jnp.float32)
    return total.astype(jnp.bfloat16)


def solution(mesh):
    return jax.shard_map(
        shards,
        mesh=mesh,
        in_specs=(
            P(("tm", "head"), None),
            P("tm", "head"),
            P("tm", "head"),
            P("tm", "head"),
            P("tm", "head"),
            P("tm", "head"),
            P("head", "tm"),
        ),
        out_specs=P(("tm", "head"), None),
        check_vma=False,
    )
```

```python
import jax
import jax.numpy as jnp
from jax import lax
from jax.sharding import PartitionSpec as P

HEAD_DIM = 128
BLOCK = 512
PAD_ROWS = 8


def gather_by_exchange(part, axis):
    count = lax.axis_size(axis)
    copies = jnp.broadcast_to(part[None], (count,) + part.shape)
    return lax.all_to_all(copies, axis, 0, 0, tiled=False)


def fold_in(earlier, later):
    return (earlier[0] + later[0], jnp.exp(later[0])[:, None, None] * earlier[1] + later[1])


def shift_along(value, axis, pairs):
    heads_here = value[1].shape[0]
    extra = jnp.broadcast_to(value[0][:, None, None], (heads_here, PAD_ROWS, HEAD_DIM))
    moved = lax.ppermute(jnp.concatenate([value[1], extra], axis=1), axis, pairs)
    return (moved[:, HEAD_DIM, 0], moved[:, :HEAD_DIM, :])


def prior_state(local_final, log_total, axis):
    units = lax.axis_size(axis)
    chips = units // 2
    parity = lax.axis_index(axis) % 2
    own = (log_total, local_final)
    partner = shift_along(own, axis, [(t, t ^ 1) for t in range(units)])
    first = jax.tree.map(lambda a, b: jnp.where(parity == 0, a, b), own, partner)
    second = jax.tree.map(lambda a, b: jnp.where(parity == 0, b, a), own, partner)
    chip_total = fold_in(first, second)

    def from_chips_back(value, gap):
        pairs = [(2 * z + c, 2 * (z + gap) + c) for z in range(chips - gap) for c in range(2)]
        return shift_along(value, axis, pairs)

    entering = fold_in(from_chips_back(chip_total, 2), from_chips_back(chip_total, 1))
    gap = 2
    while gap < chips:
        entering = fold_in(from_chips_back(entering, gap), entering)
        gap *= 2
    with_first = fold_in(entering, first)
    return jnp.where(parity == 0, entering[1], with_first[1])


def shards(frames, log_decay, w_query, w_key, w_value, w_gate, w_out):
    head_width = w_query.shape[1]
    stacked = lax.all_gather(
        jnp.concatenate([w_query, w_key, w_value, w_gate, w_out], axis=1), "tm", axis=0, tiled=True
    )
    joined = stacked[:, : 4 * head_width]
    out_blocks = stacked[:, 4 * head_width :].reshape(-1, head_width, w_out.shape[1])
    frames_here = gather_by_exchange(frames, "head").reshape(-1, frames.shape[1])
    projected = jnp.dot(
        frames_here,
        joined,
        preferred_element_type=jnp.float32,
    )
    local_len = projected.shape[0]
    heads_here = head_width // HEAD_DIM
    block_count = local_len // BLOCK
    query_blocks = (
        projected[:, :head_width]
        .astype(jnp.bfloat16)
        .reshape(block_count, BLOCK, heads_here, HEAD_DIM)
    )
    key_blocks = (
        projected[:, head_width : 2 * head_width]
        .astype(jnp.bfloat16)
        .reshape(block_count, BLOCK, heads_here, HEAD_DIM)
    )
    value_blocks = (
        projected[:, 2 * head_width : 3 * head_width]
        .astype(jnp.bfloat16)
        .reshape(block_count, BLOCK, heads_here, HEAD_DIM)
    )
    gate_all = projected[:, 3 * head_width :]
    running_blocks = jnp.cumsum(log_decay.reshape(block_count, BLOCK, heads_here), axis=1)
    slice_ordinal = jnp.arange(BLOCK, dtype=jnp.int32)
    causal = slice_ordinal[:, None] >= slice_ordinal[None, :]

    def local_step(carry_state, inputs):
        query_block, key_block, value_block, running = inputs
        gaps = running.T[:, :, None] - running.T[:, None, :]
        decay = jnp.exp(jnp.where(causal[None], gaps, -jnp.inf))
        scores = jnp.einsum(
            "thd,shd->hts", query_block, key_block, preferred_element_type=jnp.float32
        )
        weights = (scores * decay).astype(jnp.bfloat16)
        intra = jnp.einsum("hts,shd->thd", weights, value_block, preferred_element_type=jnp.float32)
        scaled = (
            key_block.astype(jnp.float32) * jnp.exp(running[-1][None, :] - running)[:, :, None]
        ).astype(jnp.bfloat16)
        update = jnp.einsum("shd,she->hde", scaled, value_block, preferred_element_type=jnp.float32)
        next_state = jnp.exp(running[-1])[:, None, None] * carry_state + update
        return (next_state, (intra, carry_state))

    zero_state = jnp.zeros((heads_here, HEAD_DIM, HEAD_DIM), jnp.float32)
    local_final, (intra_all, local_starts) = lax.scan(
        local_step, zero_state, (query_blocks, key_blocks, value_blocks, running_blocks)
    )
    prior = prior_state(local_final, jnp.sum(log_decay, axis=0), "tm")
    block_logs = running_blocks[:, -1, :]
    before = jnp.cumsum(block_logs, axis=0) - block_logs
    start_states = jnp.exp(before)[:, :, None, None] * prior[None] + local_starts
    lifted = query_blocks.astype(jnp.float32) * jnp.exp(running_blocks)[..., None]
    inter = jnp.einsum("cthd,chde->cthe", lifted, start_states, precision=lax.Precision.HIGHEST)
    retained = (intra_all + inter).reshape(local_len, heads_here, HEAD_DIM)
    center = jnp.mean(retained, axis=-1, keepdims=True)
    spread = jnp.mean((retained - center) ** 2, axis=-1, keepdims=True)
    normed = (retained - center) / jnp.sqrt(spread + 1e-05)
    gated = (
        (jax.nn.silu(gate_all.reshape(local_len, heads_here, HEAD_DIM)) * normed)
        .astype(jnp.bfloat16)
        .reshape(local_len, head_width)
    )
    heads = lax.axis_size("head")
    side = int(round(heads ** 0.5))
    me = lax.axis_index("head")
    row, col = me // side, me % side
    rows_mine = out_blocks
    by_owner = gated.reshape(side, side, local_len // heads, head_width)
    units = lax.axis_size("tm")
    half = rows_mine.shape[0] // 2
    parity = lax.axis_index("tm") % 2
    own_half = lax.dynamic_slice_in_dim(rows_mine, parity * half, half, axis=0)
    pieces = [lax.dynamic_index_in_dim(by_owner, col, axis=1, keepdims=False)]
    fetched = []
    for shift in range(1, side):
        across = [(h, (h // side) * side + (h % side + shift) % side) for h in range(heads)]
        piece = lax.dynamic_index_in_dim(by_owner, (col + shift) % side, axis=1, keepdims=False)
        pieces.append(lax.ppermute(piece, "head", across))
        fetched.append(lax.ppermute(own_half, "head", across))
    fetched = jnp.stack(fetched)
    swapped = lax.ppermute(fetched, "tm", [(t, t ^ 1) for t in range(units)])
    first = jnp.where(parity == 0, fetched, swapped)
    second = jnp.where(parity == 0, swapped, fetched)
    remote = jnp.concatenate([first, second], axis=1)
    weights_in = [rows_mine] + [remote[s] for s in range(side - 1)]
    partial = jnp.einsum(
        "syfr,skrc->yfkc",
        jnp.stack(pieces),
        jnp.stack(weights_in),
        preferred_element_type=jnp.float32,
    ).astype(jnp.bfloat16)
    partial = partial.reshape(side, local_len // heads, -1)
    total = lax.dynamic_index_in_dim(partial, row, axis=0, keepdims=False).astype(jnp.float32)
    for shift in range(1, side):
        down = [(h, ((h // side + shift) % side) * side + h % side) for h in range(heads)]
        piece = lax.dynamic_index_in_dim(partial, (row + shift) % side, axis=0, keepdims=False)
        total = total + lax.ppermute(piece, "head", down).astype(jnp.float32)
    return total.astype(jnp.bfloat16)


def solution(mesh):
    return jax.shard_map(
        shards,
        mesh=mesh,
        in_specs=(
            P(("tm", "head"), None),
            P("tm", "head"),
            P("tm", "head"),
            P("tm", "head"),
            P("tm", "head"),
            P("tm", "head"),
            P("head", "tm"),
        ),
        out_specs=P(("tm", "head"), None),
        check_vma=False,
    )
```

```python
import jax
import jax.numpy as jnp
from jax import lax
from jax.sharding import PartitionSpec as P

HEAD_DIM = 128
BLOCK = 512
PAD_ROWS = 8


def gather_by_exchange(part, axis):
    count = lax.axis_size(axis)
    copies = jnp.broadcast_to(part[None], (count,) + part.shape)
    return lax.all_to_all(copies, axis, 0, 0, tiled=False)


def prior_state(local_final, log_total, axis):
    heads_here = local_final.shape[0]
    high = log_total.astype(jnp.bfloat16)
    low = (log_total - high.astype(jnp.float32)).astype(jnp.bfloat16)
    extra = jnp.concatenate(
        [
            jnp.broadcast_to(high[:, None, None], (heads_here, 1, HEAD_DIM)),
            jnp.broadcast_to(low[:, None, None], (heads_here, 1, HEAD_DIM)),
            jnp.zeros((heads_here, PAD_ROWS - 2, HEAD_DIM), jnp.bfloat16),
        ],
        axis=1,
    )
    packed = jnp.concatenate([local_final.astype(jnp.bfloat16), extra], axis=1)
    gathered = gather_by_exchange(packed, axis)
    finals = gathered[:, :, :HEAD_DIM, :].astype(jnp.float32)
    totals = gathered[:, :, HEAD_DIM, 0].astype(jnp.float32) + gathered[:, :, HEAD_DIM + 1, 0].astype(
        jnp.float32
    )
    count = gathered.shape[0]
    mine = lax.axis_index(axis)
    order = jnp.arange(count, dtype=jnp.int32)
    between = (order[:, None] < order[None, :]) & (order[None, :] < mine)
    exponent = jnp.sum(jnp.where(between[:, :, None], totals[None, :, :], 0.0), axis=1)
    weight = jnp.where((order < mine)[:, None], jnp.exp(exponent), 0.0)
    return jnp.sum(weight[:, :, None, None] * finals, axis=0)


def shards(frames, log_decay, w_query, w_key, w_value, w_gate, w_out):
    head_width = w_query.shape[1]
    stacked = lax.all_gather(
        jnp.concatenate([w_key, w_value, w_query, w_gate, w_out], axis=1), "tm", axis=0, tiled=True
    )
    out_blocks = stacked[:, 4 * head_width :].reshape(-1, head_width, w_out.shape[1])
    frames_here = gather_by_exchange(frames, "head").reshape(-1, frames.shape[1])
    key_value = jnp.dot(
        frames_here, stacked[:, : 2 * head_width], preferred_element_type=jnp.float32
    )
    query_gate = jnp.dot(
        frames_here, stacked[:, 2 * head_width : 4 * head_width], preferred_element_type=jnp.float32
    )
    local_len = key_value.shape[0]
    heads_here = head_width // HEAD_DIM
    block_count = local_len // BLOCK
    query_blocks = (
        query_gate[:, :head_width]
        .astype(jnp.bfloat16)
        .reshape(block_count, BLOCK, heads_here, HEAD_DIM)
    )
    key_blocks = (
        key_value[:, :head_width]
        .astype(jnp.bfloat16)
        .reshape(block_count, BLOCK, heads_here, HEAD_DIM)
    )
    value_blocks = (
        key_value[:, head_width:]
        .astype(jnp.bfloat16)
        .reshape(block_count, BLOCK, heads_here, HEAD_DIM)
    )
    gate_all = query_gate[:, head_width:]
    running_blocks = jnp.cumsum(log_decay.reshape(block_count, BLOCK, heads_here), axis=1)
    slice_ordinal = jnp.arange(BLOCK, dtype=jnp.int32)
    causal = slice_ordinal[:, None] >= slice_ordinal[None, :]

    def local_step(carry_state, inputs):
        query_block, key_block, value_block, running = inputs
        gaps = running.T[:, :, None] - running.T[:, None, :]
        decay = jnp.exp(jnp.where(causal[None], gaps, -jnp.inf))
        scores = jnp.einsum(
            "thd,shd->hts", query_block, key_block, preferred_element_type=jnp.float32
        )
        weights = (scores * decay).astype(jnp.bfloat16)
        intra = jnp.einsum("hts,shd->thd", weights, value_block, preferred_element_type=jnp.float32)
        scaled = (
            key_block.astype(jnp.float32) * jnp.exp(running[-1][None, :] - running)[:, :, None]
        ).astype(jnp.bfloat16)
        update = jnp.einsum("shd,she->hde", scaled, value_block, preferred_element_type=jnp.float32)
        next_state = jnp.exp(running[-1])[:, None, None] * carry_state + update
        return (next_state, (intra, carry_state))

    zero_state = jnp.zeros((heads_here, HEAD_DIM, HEAD_DIM), jnp.float32)
    local_final, (intra_all, local_starts) = lax.scan(
        local_step, zero_state, (query_blocks, key_blocks, value_blocks, running_blocks)
    )
    prior = prior_state(local_final, jnp.sum(log_decay, axis=0), "tm")
    block_logs = running_blocks[:, -1, :]
    before = jnp.cumsum(block_logs, axis=0) - block_logs
    start_states = jnp.exp(before)[:, :, None, None] * prior[None] + local_starts
    lifted = query_blocks.astype(jnp.float32) * jnp.exp(running_blocks)[..., None]
    inter = jnp.einsum("cthd,chde->cthe", lifted, start_states, precision=lax.Precision.HIGHEST)
    retained = (intra_all + inter).reshape(local_len, heads_here, HEAD_DIM)
    center = jnp.mean(retained, axis=-1, keepdims=True)
    spread = jnp.mean((retained - center) ** 2, axis=-1, keepdims=True)
    normed = (retained - center) / jnp.sqrt(spread + 1e-05)
    gated = (
        (jax.nn.silu(gate_all.reshape(local_len, heads_here, HEAD_DIM)) * normed)
        .astype(jnp.bfloat16)
        .reshape(local_len, head_width)
    )
    heads = lax.axis_size("head")
    side = int(round(heads ** 0.5))
    me = lax.axis_index("head")
    row, col = me // side, me % side
    rows_mine = out_blocks
    by_owner = gated.reshape(side, side, local_len // heads, head_width)
    units = lax.axis_size("tm")
    half = rows_mine.shape[0] // 2
    parity = lax.axis_index("tm") % 2
    own_half = lax.dynamic_slice_in_dim(rows_mine, parity * half, half, axis=0)
    pieces = [lax.dynamic_index_in_dim(by_owner, col, axis=1, keepdims=False)]
    fetched = []
    for shift in range(1, side):
        across = [(h, (h // side) * side + (h % side + shift) % side) for h in range(heads)]
        piece = lax.dynamic_index_in_dim(by_owner, (col + shift) % side, axis=1, keepdims=False)
        pieces.append(lax.ppermute(piece, "head", across))
        fetched.append(lax.ppermute(own_half, "head", across))
    fetched = jnp.stack(fetched)
    swapped = lax.ppermute(fetched, "tm", [(t, t ^ 1) for t in range(units)])
    first = jnp.where(parity == 0, fetched, swapped)
    second = jnp.where(parity == 0, swapped, fetched)
    remote = jnp.concatenate([first, second], axis=1)
    weights_in = [rows_mine] + [remote[s] for s in range(side - 1)]
    partial = jnp.einsum(
        "syfr,skrc->yfkc",
        jnp.stack(pieces),
        jnp.stack(weights_in),
        preferred_element_type=jnp.float32,
    ).astype(jnp.bfloat16)
    partial = partial.reshape(side, local_len // heads, -1)
    total = lax.dynamic_index_in_dim(partial, row, axis=0, keepdims=False).astype(jnp.float32)
    for shift in range(1, side):
        down = [(h, ((h // side + shift) % side) * side + h % side) for h in range(heads)]
        piece = lax.dynamic_index_in_dim(partial, (row + shift) % side, axis=0, keepdims=False)
        total = total + lax.ppermute(piece, "head", down).astype(jnp.float32)
    return total.astype(jnp.bfloat16)


def solution(mesh):
    return jax.shard_map(
        shards,
        mesh=mesh,
        in_specs=(
            P(("tm", "head"), None),
            P("tm", "head"),
            P("tm", "head"),
            P("tm", "head"),
            P("tm", "head"),
            P("tm", "head"),
            P("head", "tm"),
        ),
        out_specs=P(("tm", "head"), None),
        check_vma=False,
    )
```

```python
import jax
import jax.numpy as jnp
from jax import lax
from jax.sharding import PartitionSpec as P

HEAD_DIM = 128
BLOCK = 512
PAD_ROWS = 8


def gather_by_exchange(part, axis, groups=None):
    count = lax.axis_size(axis) if groups is None else len(groups[0])
    copies = jnp.broadcast_to(part[None], (count,) + part.shape)
    return lax.all_to_all(copies, axis, 0, 0, tiled=False, axis_index_groups=groups)


def pack_state(state, log_total):
    heads_here = state.shape[0]
    high = log_total.astype(jnp.bfloat16)
    low = (log_total - high.astype(jnp.float32)).astype(jnp.bfloat16)
    extra = jnp.concatenate(
        [
            jnp.broadcast_to(high[:, None, None], (heads_here, 1, HEAD_DIM)),
            jnp.broadcast_to(low[:, None, None], (heads_here, 1, HEAD_DIM)),
            jnp.zeros((heads_here, PAD_ROWS - 2, HEAD_DIM), jnp.bfloat16),
        ],
        axis=1,
    )
    return jnp.concatenate([state.astype(jnp.bfloat16), extra], axis=1)


def prior_state(local_final, log_total, axis):
    units = lax.axis_size(axis)
    heads_here = local_final.shape[0]
    parity = lax.axis_index(axis) % 2
    chip = lax.axis_index(axis) // 2
    extra = jnp.broadcast_to(log_total[:, None, None], (heads_here, PAD_ROWS, HEAD_DIM))
    moved = lax.ppermute(
        jnp.concatenate([local_final, extra], axis=1), axis, [(t, t ^ 1) for t in range(units)]
    )
    partner_state, partner_total = moved[:, :HEAD_DIM, :], moved[:, HEAD_DIM, 0]
    first_state = jnp.where(parity == 0, local_final, partner_state)
    first_total = jnp.where(parity == 0, log_total, partner_total)
    second_state = jnp.where(parity == 0, partner_state, local_final)
    second_total = jnp.where(parity == 0, partner_total, log_total)
    chip_state = jnp.exp(second_total)[:, None, None] * first_state + second_state
    chip_total = first_total + second_total
    same_place = [[t for t in range(units) if t % 2 == p] for p in range(2)]
    gathered = gather_by_exchange(pack_state(chip_state, chip_total), axis, same_place)
    finals = gathered[:, :, :HEAD_DIM, :].astype(jnp.float32)
    totals = gathered[:, :, HEAD_DIM, 0].astype(jnp.float32) + gathered[:, :, HEAD_DIM + 1, 0].astype(
        jnp.float32
    )
    count = gathered.shape[0]
    order = jnp.arange(count, dtype=jnp.int32)
    between = (order[:, None] < order[None, :]) & (order[None, :] < chip)
    exponent = jnp.sum(jnp.where(between[:, :, None], totals[None, :, :], 0.0), axis=1)
    weight = jnp.where((order < chip)[:, None], jnp.exp(exponent), 0.0)
    entering = jnp.sum(weight[:, :, None, None] * finals, axis=0)
    with_first = jnp.exp(first_total)[:, None, None] * entering + first_state
    return jnp.where(parity == 0, entering, with_first)


def shards(frames, log_decay, w_query, w_key, w_value, w_gate, w_out):
    head_width = w_query.shape[1]
    stacked = lax.all_gather(
        jnp.concatenate([w_query, w_key, w_value, w_gate, w_out], axis=1), "tm", axis=0, tiled=True
    )
    joined = stacked[:, : 4 * head_width]
    out_blocks = stacked[:, 4 * head_width :].reshape(-1, head_width, w_out.shape[1])
    frames_here = gather_by_exchange(frames, "head").reshape(-1, frames.shape[1])
    projected = jnp.dot(
        frames_here,
        joined,
        preferred_element_type=jnp.float32,
    )
    local_len = projected.shape[0]
    heads_here = head_width // HEAD_DIM
    block_count = local_len // BLOCK
    query_blocks = (
        projected[:, :head_width]
        .astype(jnp.bfloat16)
        .reshape(block_count, BLOCK, heads_here, HEAD_DIM)
    )
    key_blocks = (
        projected[:, head_width : 2 * head_width]
        .astype(jnp.bfloat16)
        .reshape(block_count, BLOCK, heads_here, HEAD_DIM)
    )
    value_blocks = (
        projected[:, 2 * head_width : 3 * head_width]
        .astype(jnp.bfloat16)
        .reshape(block_count, BLOCK, heads_here, HEAD_DIM)
    )
    gate_all = projected[:, 3 * head_width :]
    running_blocks = jnp.cumsum(log_decay.reshape(block_count, BLOCK, heads_here), axis=1)
    slice_ordinal = jnp.arange(BLOCK, dtype=jnp.int32)
    causal = slice_ordinal[:, None] >= slice_ordinal[None, :]

    def local_step(carry_state, inputs):
        query_block, key_block, value_block, running = inputs
        gaps = running.T[:, :, None] - running.T[:, None, :]
        decay = jnp.exp(jnp.where(causal[None], gaps, -jnp.inf))
        scores = jnp.einsum(
            "thd,shd->hts", query_block, key_block, preferred_element_type=jnp.float32
        )
        weights = (scores * decay).astype(jnp.bfloat16)
        intra = jnp.einsum("hts,shd->thd", weights, value_block, preferred_element_type=jnp.float32)
        scaled = (
            key_block.astype(jnp.float32) * jnp.exp(running[-1][None, :] - running)[:, :, None]
        ).astype(jnp.bfloat16)
        update = jnp.einsum("shd,she->hde", scaled, value_block, preferred_element_type=jnp.float32)
        next_state = jnp.exp(running[-1])[:, None, None] * carry_state + update
        return (next_state, (intra, carry_state))

    zero_state = jnp.zeros((heads_here, HEAD_DIM, HEAD_DIM), jnp.float32)
    local_final, (intra_all, local_starts) = lax.scan(
        local_step, zero_state, (query_blocks, key_blocks, value_blocks, running_blocks)
    )
    prior = prior_state(local_final, jnp.sum(log_decay, axis=0), "tm")
    block_logs = running_blocks[:, -1, :]
    before = jnp.cumsum(block_logs, axis=0) - block_logs
    start_states = jnp.exp(before)[:, :, None, None] * prior[None] + local_starts
    lifted = query_blocks.astype(jnp.float32) * jnp.exp(running_blocks)[..., None]
    inter = jnp.einsum("cthd,chde->cthe", lifted, start_states, precision=lax.Precision.HIGHEST)
    retained = (intra_all + inter).reshape(local_len, heads_here, HEAD_DIM)
    center = jnp.mean(retained, axis=-1, keepdims=True)
    spread = jnp.mean((retained - center) ** 2, axis=-1, keepdims=True)
    normed = (retained - center) / jnp.sqrt(spread + 1e-05)
    gated = (
        (jax.nn.silu(gate_all.reshape(local_len, heads_here, HEAD_DIM)) * normed)
        .astype(jnp.bfloat16)
        .reshape(local_len, head_width)
    )
    heads = lax.axis_size("head")
    side = int(round(heads ** 0.5))
    me = lax.axis_index("head")
    row, col = me // side, me % side
    rows_mine = out_blocks
    by_owner = gated.reshape(side, side, local_len // heads, head_width)
    units = lax.axis_size("tm")
    half = rows_mine.shape[0] // 2
    parity = lax.axis_index("tm") % 2
    own_half = lax.dynamic_slice_in_dim(rows_mine, parity * half, half, axis=0)
    pieces = [lax.dynamic_index_in_dim(by_owner, col, axis=1, keepdims=False)]
    fetched = []
    for shift in range(1, side):
        across = [(h, (h // side) * side + (h % side + shift) % side) for h in range(heads)]
        piece = lax.dynamic_index_in_dim(by_owner, (col + shift) % side, axis=1, keepdims=False)
        pieces.append(lax.ppermute(piece, "head", across))
        fetched.append(lax.ppermute(own_half, "head", across))
    fetched = jnp.stack(fetched)
    swapped = lax.ppermute(fetched, "tm", [(t, t ^ 1) for t in range(units)])
    first = jnp.where(parity == 0, fetched, swapped)
    second = jnp.where(parity == 0, swapped, fetched)
    remote = jnp.concatenate([first, second], axis=1)
    weights_in = [rows_mine] + [remote[s] for s in range(side - 1)]
    partial = jnp.einsum(
        "syfr,skrc->yfkc",
        jnp.stack(pieces),
        jnp.stack(weights_in),
        preferred_element_type=jnp.float32,
    ).astype(jnp.bfloat16)
    partial = partial.reshape(side, local_len // heads, -1)
    total = lax.dynamic_index_in_dim(partial, row, axis=0, keepdims=False).astype(jnp.float32)
    for shift in range(1, side):
        down = [(h, ((h // side + shift) % side) * side + h % side) for h in range(heads)]
        piece = lax.dynamic_index_in_dim(partial, (row + shift) % side, axis=0, keepdims=False)
        total = total + lax.ppermute(piece, "head", down).astype(jnp.float32)
    return total.astype(jnp.bfloat16)


def solution(mesh):
    return jax.shard_map(
        shards,
        mesh=mesh,
        in_specs=(
            P(("tm", "head"), None),
            P("tm", "head"),
            P("tm", "head"),
            P("tm", "head"),
            P("tm", "head"),
            P("tm", "head"),
            P("head", "tm"),
        ),
        out_specs=P(("tm", "head"), None),
        check_vma=False,
    )
```

```python
import jax
import jax.numpy as jnp
from jax import lax
from jax.sharding import PartitionSpec as P

HEAD_DIM = 128
BLOCK = 512
PAD_ROWS = 8


def gather_by_exchange(part, axis):
    count = lax.axis_size(axis)
    copies = jnp.broadcast_to(part[None], (count,) + part.shape)
    return lax.all_to_all(copies, axis, 0, 0, tiled=False)


def prior_state(local_final, log_total, axis):
    heads_here = local_final.shape[0]
    high = log_total.astype(jnp.bfloat16)
    low = (log_total - high.astype(jnp.float32)).astype(jnp.bfloat16)
    extra = jnp.concatenate(
        [
            jnp.broadcast_to(high[:, None, None], (heads_here, 1, HEAD_DIM)),
            jnp.broadcast_to(low[:, None, None], (heads_here, 1, HEAD_DIM)),
            jnp.zeros((heads_here, PAD_ROWS - 2, HEAD_DIM), jnp.bfloat16),
        ],
        axis=1,
    )
    packed = jnp.concatenate([local_final.astype(jnp.bfloat16), extra], axis=1)
    gathered = gather_by_exchange(packed, axis)
    finals = gathered[:, :, :HEAD_DIM, :].astype(jnp.float32)
    totals = gathered[:, :, HEAD_DIM, 0].astype(jnp.float32) + gathered[:, :, HEAD_DIM + 1, 0].astype(
        jnp.float32
    )
    count = gathered.shape[0]
    mine = lax.axis_index(axis)
    order = jnp.arange(count, dtype=jnp.int32)
    between = (order[:, None] < order[None, :]) & (order[None, :] < mine)
    exponent = jnp.sum(jnp.where(between[:, :, None], totals[None, :, :], 0.0), axis=1)
    weight = jnp.where((order < mine)[:, None], jnp.exp(exponent), 0.0)
    return jnp.sum(weight[:, :, None, None] * finals, axis=0)


def shards(frames, log_decay, w_query, w_key, w_value, w_gate, w_out):
    head_width = w_query.shape[1]
    blocks = [w_query, w_key, w_value, w_gate, w_out]
    width = sum(block.shape[1] for block in blocks)
    packed = sum(
        jnp.pad(block, ((0, 0), (start, width - start - block.shape[1])))
        for start, block in zip(range(0, width, head_width), blocks)
    )
    stacked = lax.all_gather(packed, "tm", axis=0, tiled=True)
    joined = stacked[:, : 4 * head_width]
    out_blocks = stacked[:, 4 * head_width :].reshape(-1, head_width, w_out.shape[1])
    frames_here = gather_by_exchange(frames, "head").reshape(-1, frames.shape[1])
    projected = jnp.dot(
        frames_here,
        joined,
        preferred_element_type=jnp.float32,
    )
    local_len = projected.shape[0]
    heads_here = head_width // HEAD_DIM
    block_count = local_len // BLOCK
    query_blocks = (
        projected[:, :head_width]
        .astype(jnp.bfloat16)
        .reshape(block_count, BLOCK, heads_here, HEAD_DIM)
    )
    key_blocks = (
        projected[:, head_width : 2 * head_width]
        .astype(jnp.bfloat16)
        .reshape(block_count, BLOCK, heads_here, HEAD_DIM)
    )
    value_blocks = (
        projected[:, 2 * head_width : 3 * head_width]
        .astype(jnp.bfloat16)
        .reshape(block_count, BLOCK, heads_here, HEAD_DIM)
    )
    gate_all = projected[:, 3 * head_width :]
    running_blocks = jnp.cumsum(log_decay.reshape(block_count, BLOCK, heads_here), axis=1)
    slice_ordinal = jnp.arange(BLOCK, dtype=jnp.int32)
    causal = slice_ordinal[:, None] >= slice_ordinal[None, :]

    def local_step(carry_state, inputs):
        query_block, key_block, value_block, running = inputs
        gaps = running.T[:, :, None] - running.T[:, None, :]
        decay = jnp.exp(jnp.where(causal[None], gaps, -jnp.inf))
        scores = jnp.einsum(
            "thd,shd->hts", query_block, key_block, preferred_element_type=jnp.float32
        )
        weights = (scores * decay).astype(jnp.bfloat16)
        intra = jnp.einsum("hts,shd->thd", weights, value_block, preferred_element_type=jnp.float32)
        scaled = (
            key_block.astype(jnp.float32) * jnp.exp(running[-1][None, :] - running)[:, :, None]
        ).astype(jnp.bfloat16)
        update = jnp.einsum("shd,she->hde", scaled, value_block, preferred_element_type=jnp.float32)
        next_state = jnp.exp(running[-1])[:, None, None] * carry_state + update
        return (next_state, (intra, carry_state))

    zero_state = jnp.zeros((heads_here, HEAD_DIM, HEAD_DIM), jnp.float32)
    local_final, (intra_all, local_starts) = lax.scan(
        local_step, zero_state, (query_blocks, key_blocks, value_blocks, running_blocks)
    )
    prior = prior_state(local_final, jnp.sum(log_decay, axis=0), "tm")
    block_logs = running_blocks[:, -1, :]
    before = jnp.cumsum(block_logs, axis=0) - block_logs
    start_states = jnp.exp(before)[:, :, None, None] * prior[None] + local_starts
    lifted = query_blocks.astype(jnp.float32) * jnp.exp(running_blocks)[..., None]
    inter = jnp.einsum("cthd,chde->cthe", lifted, start_states, precision=lax.Precision.HIGHEST)
    retained = (intra_all + inter).reshape(local_len, heads_here, HEAD_DIM)
    center = jnp.mean(retained, axis=-1, keepdims=True)
    spread = jnp.mean((retained - center) ** 2, axis=-1, keepdims=True)
    normed = (retained - center) / jnp.sqrt(spread + 1e-05)
    gated = (
        (jax.nn.silu(gate_all.reshape(local_len, heads_here, HEAD_DIM)) * normed)
        .astype(jnp.bfloat16)
        .reshape(local_len, head_width)
    )
    heads = lax.axis_size("head")
    side = int(round(heads ** 0.5))
    me = lax.axis_index("head")
    row, col = me // side, me % side
    rows_mine = out_blocks
    by_owner = gated.reshape(side, side, local_len // heads, head_width)
    units = lax.axis_size("tm")
    half = rows_mine.shape[0] // 2
    parity = lax.axis_index("tm") % 2
    own_half = lax.dynamic_slice_in_dim(rows_mine, parity * half, half, axis=0)
    pieces = [lax.dynamic_index_in_dim(by_owner, col, axis=1, keepdims=False)]
    fetched = []
    for shift in range(1, side):
        across = [(h, (h // side) * side + (h % side + shift) % side) for h in range(heads)]
        piece = lax.dynamic_index_in_dim(by_owner, (col + shift) % side, axis=1, keepdims=False)
        pieces.append(lax.ppermute(piece, "head", across))
        fetched.append(lax.ppermute(own_half, "head", across))
    fetched = jnp.stack(fetched)
    swapped = lax.ppermute(fetched, "tm", [(t, t ^ 1) for t in range(units)])
    first = jnp.where(parity == 0, fetched, swapped)
    second = jnp.where(parity == 0, swapped, fetched)
    remote = jnp.concatenate([first, second], axis=1)
    weights_in = [rows_mine] + [remote[s] for s in range(side - 1)]
    partial = jnp.einsum(
        "syfr,skrc->yfkc",
        jnp.stack(pieces),
        jnp.stack(weights_in),
        preferred_element_type=jnp.float32,
    ).astype(jnp.bfloat16)
    partial = partial.reshape(side, local_len // heads, -1)
    total = lax.dynamic_index_in_dim(partial, row, axis=0, keepdims=False).astype(jnp.float32)
    for shift in range(1, side):
        down = [(h, ((h // side + shift) % side) * side + h % side) for h in range(heads)]
        piece = lax.dynamic_index_in_dim(partial, (row + shift) % side, axis=0, keepdims=False)
        total = total + lax.ppermute(piece, "head", down).astype(jnp.float32)
    return total.astype(jnp.bfloat16)


def solution(mesh):
    return jax.shard_map(
        shards,
        mesh=mesh,
        in_specs=(
            P(("tm", "head"), None),
            P("tm", "head"),
            P("tm", "head"),
            P("tm", "head"),
            P("tm", "head"),
            P("tm", "head"),
            P("head", "tm"),
        ),
        out_specs=P(("tm", "head"), None),
        check_vma=False,
    )
```

```python
import jax
import jax.numpy as jnp
from jax import lax
from jax.sharding import PartitionSpec as P

HEAD_DIM = 128
BLOCK = 512
PAD_ROWS = 8


def gather_by_exchange(part, axis):
    count = lax.axis_size(axis)
    copies = jnp.broadcast_to(part[None], (count,) + part.shape)
    return lax.all_to_all(copies, axis, 0, 0, tiled=False)


def prior_state(local_final, log_total, axis):
    heads_here = local_final.shape[0]
    high = log_total.astype(jnp.bfloat16)
    low = (log_total - high.astype(jnp.float32)).astype(jnp.bfloat16)
    extra = jnp.concatenate(
        [
            jnp.broadcast_to(high[:, None, None], (heads_here, 1, HEAD_DIM)),
            jnp.broadcast_to(low[:, None, None], (heads_here, 1, HEAD_DIM)),
            jnp.zeros((heads_here, PAD_ROWS - 2, HEAD_DIM), jnp.bfloat16),
        ],
        axis=1,
    )
    packed = jnp.concatenate([local_final.astype(jnp.bfloat16), extra], axis=1)
    gathered = gather_by_exchange(packed, axis)
    finals = gathered[:, :, :HEAD_DIM, :].astype(jnp.float32)
    totals = gathered[:, :, HEAD_DIM, 0].astype(jnp.float32) + gathered[:, :, HEAD_DIM + 1, 0].astype(
        jnp.float32
    )
    count = gathered.shape[0]
    mine = lax.axis_index(axis)
    order = jnp.arange(count, dtype=jnp.int32)
    between = (order[:, None] < order[None, :]) & (order[None, :] < mine)
    exponent = jnp.sum(jnp.where(between[:, :, None], totals[None, :, :], 0.0), axis=1)
    weight = jnp.where((order < mine)[:, None], jnp.exp(exponent), 0.0)
    return jnp.sum(weight[:, :, None, None] * finals, axis=0)


def shards(frames, log_decay, w_query, w_key, w_value, w_gate, w_out):
    head_width = w_query.shape[1]
    blocks = [w_key, w_value, w_query, w_gate, w_out]
    width = sum(block.shape[1] for block in blocks)
    packed = sum(
        jnp.pad(block, ((0, 0), (start, width - start - block.shape[1])))
        for start, block in zip(range(0, width, head_width), blocks)
    )
    stacked = lax.all_gather(packed, "tm", axis=0, tiled=True)
    out_blocks = stacked[:, 4 * head_width :].reshape(-1, head_width, w_out.shape[1])
    frames_here = gather_by_exchange(frames, "head").reshape(-1, frames.shape[1])
    key_value = jnp.dot(
        frames_here, stacked[:, : 2 * head_width], preferred_element_type=jnp.float32
    )
    query_gate = jnp.dot(
        frames_here, stacked[:, 2 * head_width : 4 * head_width], preferred_element_type=jnp.float32
    )
    local_len = key_value.shape[0]
    heads_here = head_width // HEAD_DIM
    block_count = local_len // BLOCK
    query_blocks = (
        query_gate[:, :head_width]
        .astype(jnp.bfloat16)
        .reshape(block_count, BLOCK, heads_here, HEAD_DIM)
    )
    key_blocks = (
        key_value[:, :head_width]
        .astype(jnp.bfloat16)
        .reshape(block_count, BLOCK, heads_here, HEAD_DIM)
    )
    value_blocks = (
        key_value[:, head_width:]
        .astype(jnp.bfloat16)
        .reshape(block_count, BLOCK, heads_here, HEAD_DIM)
    )
    gate_all = query_gate[:, head_width:]
    running_blocks = jnp.cumsum(log_decay.reshape(block_count, BLOCK, heads_here), axis=1)
    slice_ordinal = jnp.arange(BLOCK, dtype=jnp.int32)
    causal = slice_ordinal[:, None] >= slice_ordinal[None, :]

    def local_step(carry_state, inputs):
        query_block, key_block, value_block, running = inputs
        gaps = running.T[:, :, None] - running.T[:, None, :]
        decay = jnp.exp(jnp.where(causal[None], gaps, -jnp.inf))
        scores = jnp.einsum(
            "thd,shd->hts", query_block, key_block, preferred_element_type=jnp.float32
        )
        weights = (scores * decay).astype(jnp.bfloat16)
        intra = jnp.einsum("hts,shd->thd", weights, value_block, preferred_element_type=jnp.float32)
        scaled = (
            key_block.astype(jnp.float32) * jnp.exp(running[-1][None, :] - running)[:, :, None]
        ).astype(jnp.bfloat16)
        update = jnp.einsum("shd,she->hde", scaled, value_block, preferred_element_type=jnp.float32)
        next_state = jnp.exp(running[-1])[:, None, None] * carry_state + update
        return (next_state, (intra, carry_state))

    zero_state = jnp.zeros((heads_here, HEAD_DIM, HEAD_DIM), jnp.float32)
    local_final, (intra_all, local_starts) = lax.scan(
        local_step, zero_state, (query_blocks, key_blocks, value_blocks, running_blocks)
    )
    prior = prior_state(local_final, jnp.sum(log_decay, axis=0), "tm")
    block_logs = running_blocks[:, -1, :]
    before = jnp.cumsum(block_logs, axis=0) - block_logs
    start_states = jnp.exp(before)[:, :, None, None] * prior[None] + local_starts
    lifted = query_blocks.astype(jnp.float32) * jnp.exp(running_blocks)[..., None]
    inter = jnp.einsum("cthd,chde->cthe", lifted, start_states, precision=lax.Precision.HIGHEST)
    retained = (intra_all + inter).reshape(local_len, heads_here, HEAD_DIM)
    center = jnp.mean(retained, axis=-1, keepdims=True)
    spread = jnp.mean((retained - center) ** 2, axis=-1, keepdims=True)
    normed = (retained - center) / jnp.sqrt(spread + 1e-05)
    gated = (
        (jax.nn.silu(gate_all.reshape(local_len, heads_here, HEAD_DIM)) * normed)
        .astype(jnp.bfloat16)
        .reshape(local_len, head_width)
    )
    heads = lax.axis_size("head")
    side = int(round(heads ** 0.5))
    me = lax.axis_index("head")
    row, col = me // side, me % side
    rows_mine = out_blocks
    by_owner = gated.reshape(side, side, local_len // heads, head_width)
    units = lax.axis_size("tm")
    half = rows_mine.shape[0] // 2
    parity = lax.axis_index("tm") % 2
    own_half = lax.dynamic_slice_in_dim(rows_mine, parity * half, half, axis=0)
    pieces = [lax.dynamic_index_in_dim(by_owner, col, axis=1, keepdims=False)]
    fetched = []
    for shift in range(1, side):
        across = [(h, (h // side) * side + (h % side + shift) % side) for h in range(heads)]
        piece = lax.dynamic_index_in_dim(by_owner, (col + shift) % side, axis=1, keepdims=False)
        pieces.append(lax.ppermute(piece, "head", across))
        fetched.append(lax.ppermute(own_half, "head", across))
    fetched = jnp.stack(fetched)
    swapped = lax.ppermute(fetched, "tm", [(t, t ^ 1) for t in range(units)])
    first = jnp.where(parity == 0, fetched, swapped)
    second = jnp.where(parity == 0, swapped, fetched)
    remote = jnp.concatenate([first, second], axis=1)
    weights_in = [rows_mine] + [remote[s] for s in range(side - 1)]
    partial = jnp.einsum(
        "syfr,skrc->yfkc",
        jnp.stack(pieces),
        jnp.stack(weights_in),
        preferred_element_type=jnp.float32,
    ).astype(jnp.bfloat16)
    partial = partial.reshape(side, local_len // heads, -1)
    total = lax.dynamic_index_in_dim(partial, row, axis=0, keepdims=False).astype(jnp.float32)
    for shift in range(1, side):
        down = [(h, ((h // side + shift) % side) * side + h % side) for h in range(heads)]
        piece = lax.dynamic_index_in_dim(partial, (row + shift) % side, axis=0, keepdims=False)
        total = total + lax.ppermute(piece, "head", down).astype(jnp.float32)
    return total.astype(jnp.bfloat16)


def solution(mesh):
    return jax.shard_map(
        shards,
        mesh=mesh,
        in_specs=(
            P(("tm", "head"), None),
            P("tm", "head"),
            P("tm", "head"),
            P("tm", "head"),
            P("tm", "head"),
            P("tm", "head"),
            P("head", "tm"),
        ),
        out_specs=P(("tm", "head"), None),
        check_vma=False,
    )
```

```python
import jax
import jax.numpy as jnp
from jax import lax
from jax.sharding import PartitionSpec as P

HEAD_DIM = 128
BLOCK = 512
PAD_ROWS = 8


def gather_by_exchange(part, axis):
    count = lax.axis_size(axis)
    copies = jnp.broadcast_to(part[None], (count,) + part.shape)
    return lax.all_to_all(copies, axis, 0, 0, tiled=False)


def prior_state(local_final, log_total, axis):
    heads_here = local_final.shape[0]
    high = log_total.astype(jnp.bfloat16)
    low = (log_total - high.astype(jnp.float32)).astype(jnp.bfloat16)
    extra = jnp.concatenate(
        [
            jnp.broadcast_to(high[:, None, None], (heads_here, 1, HEAD_DIM)),
            jnp.broadcast_to(low[:, None, None], (heads_here, 1, HEAD_DIM)),
            jnp.zeros((heads_here, PAD_ROWS - 2, HEAD_DIM), jnp.bfloat16),
        ],
        axis=1,
    )
    packed = jnp.concatenate([local_final.astype(jnp.bfloat16), extra], axis=1)
    gathered = gather_by_exchange(packed, axis)
    finals = gathered[:, :, :HEAD_DIM, :].astype(jnp.float32)
    totals = gathered[:, :, HEAD_DIM, 0].astype(jnp.float32) + gathered[:, :, HEAD_DIM + 1, 0].astype(
        jnp.float32
    )
    count = gathered.shape[0]
    mine = lax.axis_index(axis)
    order = jnp.arange(count, dtype=jnp.int32)
    between = (order[:, None] < order[None, :]) & (order[None, :] < mine)
    exponent = jnp.sum(jnp.where(between[:, :, None], totals[None, :, :], 0.0), axis=1)
    weight = jnp.where((order < mine)[:, None], jnp.exp(exponent), 0.0)
    return jnp.sum(weight[:, :, None, None] * finals, axis=0)


def shards(frames, log_decay, w_query, w_key, w_value, w_gate, w_out):
    head_width = w_query.shape[1]
    blocks = [w_query, w_key, w_value, w_gate, w_out]
    width = sum(block.shape[1] for block in blocks)
    packed = sum(
        jnp.pad(block, ((0, 0), (start, width - start - block.shape[1])))
        for start, block in zip(range(0, width, head_width), blocks)
    )
    stacked = lax.all_gather(packed, "tm", axis=0, tiled=True)
    joined = stacked[:, : 4 * head_width]
    out_blocks = stacked[:, 4 * head_width :].reshape(-1, head_width, w_out.shape[1])
    frames_here = gather_by_exchange(frames, "head").reshape(-1, frames.shape[1])
    projected = jnp.dot(
        frames_here,
        joined,
        preferred_element_type=jnp.float32,
    )
    local_len = projected.shape[0]
    heads_here = head_width // HEAD_DIM
    block_count = local_len // BLOCK
    query_blocks = (
        projected[:, :head_width]
        .astype(jnp.bfloat16)
        .reshape(block_count, BLOCK, heads_here, HEAD_DIM)
    )
    key_blocks = (
        projected[:, head_width : 2 * head_width]
        .astype(jnp.bfloat16)
        .reshape(block_count, BLOCK, heads_here, HEAD_DIM)
    )
    value_blocks = (
        projected[:, 2 * head_width : 3 * head_width]
        .astype(jnp.bfloat16)
        .reshape(block_count, BLOCK, heads_here, HEAD_DIM)
    )
    gate_all = projected[:, 3 * head_width :]
    running_blocks = jnp.cumsum(log_decay.reshape(block_count, BLOCK, heads_here), axis=1)
    slice_ordinal = jnp.arange(BLOCK, dtype=jnp.int32)
    causal = slice_ordinal[:, None] >= slice_ordinal[None, :]

    def local_step(carry_state, inputs):
        query_block, key_block, value_block, running = inputs
        gaps = running.T[:, :, None] - running.T[:, None, :]
        decay = jnp.exp(jnp.where(causal[None], gaps, -jnp.inf))
        scores = jnp.einsum(
            "thd,shd->hts", query_block, key_block, preferred_element_type=jnp.float32
        )
        weights = (scores * decay).astype(jnp.bfloat16)
        intra = jnp.einsum("hts,shd->thd", weights, value_block, preferred_element_type=jnp.float32)
        scaled = (
            key_block.astype(jnp.float32) * jnp.exp(running[-1][None, :] - running)[:, :, None]
        ).astype(jnp.bfloat16)
        update = jnp.einsum("shd,she->hde", scaled, value_block, preferred_element_type=jnp.float32)
        next_state = jnp.exp(running[-1])[:, None, None] * carry_state + update
        return (next_state, (intra, carry_state))

    zero_state = jnp.zeros((heads_here, HEAD_DIM, HEAD_DIM), jnp.float32)
    local_final, (intra_all, local_starts) = lax.scan(
        local_step, zero_state, (query_blocks, key_blocks, value_blocks, running_blocks)
    )
    prior = prior_state(local_final, jnp.sum(log_decay, axis=0), "tm")
    block_logs = running_blocks[:, -1, :]
    before = jnp.cumsum(block_logs, axis=0) - block_logs
    start_states = jnp.exp(before)[:, :, None, None] * prior[None] + local_starts
    lifted = query_blocks.astype(jnp.float32) * jnp.exp(running_blocks)[..., None]
    inter = jnp.einsum(
        "cthd,chde->cthe",
        lifted.astype(jnp.bfloat16),
        start_states.astype(jnp.bfloat16),
        preferred_element_type=jnp.float32,
    )
    retained = (intra_all + inter).reshape(local_len, heads_here, HEAD_DIM)
    center = jnp.mean(retained, axis=-1, keepdims=True)
    spread = jnp.mean((retained - center) ** 2, axis=-1, keepdims=True)
    normed = (retained - center) / jnp.sqrt(spread + 1e-05)
    gated = (
        (jax.nn.silu(gate_all.reshape(local_len, heads_here, HEAD_DIM)) * normed)
        .astype(jnp.bfloat16)
        .reshape(local_len, head_width)
    )
    heads = lax.axis_size("head")
    side = int(round(heads ** 0.5))
    me = lax.axis_index("head")
    row, col = me // side, me % side
    rows_mine = out_blocks
    by_owner = gated.reshape(side, side, local_len // heads, head_width)
    units = lax.axis_size("tm")
    half = rows_mine.shape[0] // 2
    parity = lax.axis_index("tm") % 2
    own_half = lax.dynamic_slice_in_dim(rows_mine, parity * half, half, axis=0)
    pieces = [lax.dynamic_index_in_dim(by_owner, col, axis=1, keepdims=False)]
    fetched = []
    for shift in range(1, side):
        across = [(h, (h // side) * side + (h % side + shift) % side) for h in range(heads)]
        piece = lax.dynamic_index_in_dim(by_owner, (col + shift) % side, axis=1, keepdims=False)
        pieces.append(lax.ppermute(piece, "head", across))
        fetched.append(lax.ppermute(own_half, "head", across))
    fetched = jnp.stack(fetched)
    swapped = lax.ppermute(fetched, "tm", [(t, t ^ 1) for t in range(units)])
    first = jnp.where(parity == 0, fetched, swapped)
    second = jnp.where(parity == 0, swapped, fetched)
    remote = jnp.concatenate([first, second], axis=1)
    weights_in = [rows_mine] + [remote[s] for s in range(side - 1)]
    partial = jnp.einsum(
        "syfr,skrc->yfkc",
        jnp.stack(pieces),
        jnp.stack(weights_in),
        preferred_element_type=jnp.float32,
    ).astype(jnp.bfloat16)
    partial = partial.reshape(side, local_len // heads, -1)
    total = lax.dynamic_index_in_dim(partial, row, axis=0, keepdims=False).astype(jnp.float32)
    for shift in range(1, side):
        down = [(h, ((h // side + shift) % side) * side + h % side) for h in range(heads)]
        piece = lax.dynamic_index_in_dim(partial, (row + shift) % side, axis=0, keepdims=False)
        total = total + lax.ppermute(piece, "head", down).astype(jnp.float32)
    return total.astype(jnp.bfloat16)


def solution(mesh):
    return jax.shard_map(
        shards,
        mesh=mesh,
        in_specs=(
            P(("tm", "head"), None),
            P("tm", "head"),
            P("tm", "head"),
            P("tm", "head"),
            P("tm", "head"),
            P("tm", "head"),
            P("head", "tm"),
        ),
        out_specs=P(("tm", "head"), None),
        check_vma=False,
    )
```

```python
import jax
import jax.numpy as jnp
from jax import lax
from jax.sharding import PartitionSpec as P

HEAD_DIM = 128
BLOCK = 512
PAD_ROWS = 8


def gather_by_exchange(part, axis):
    count = lax.axis_size(axis)
    copies = jnp.broadcast_to(part[None], (count,) + part.shape)
    return lax.all_to_all(copies, axis, 0, 0, tiled=False)


def prior_state(local_final, log_total, axis):
    heads_here = local_final.shape[0]
    high = log_total.astype(jnp.bfloat16)
    low = (log_total - high.astype(jnp.float32)).astype(jnp.bfloat16)
    extra = jnp.concatenate(
        [
            jnp.broadcast_to(high[:, None, None], (heads_here, 1, HEAD_DIM)),
            jnp.broadcast_to(low[:, None, None], (heads_here, 1, HEAD_DIM)),
            jnp.zeros((heads_here, PAD_ROWS - 2, HEAD_DIM), jnp.bfloat16),
        ],
        axis=1,
    )
    packed = jnp.concatenate([local_final.astype(jnp.bfloat16), extra], axis=1)
    gathered = gather_by_exchange(packed, axis)
    finals = gathered[:, :, :HEAD_DIM, :].astype(jnp.float32)
    totals = gathered[:, :, HEAD_DIM, 0].astype(jnp.float32) + gathered[:, :, HEAD_DIM + 1, 0].astype(
        jnp.float32
    )
    count = gathered.shape[0]
    mine = lax.axis_index(axis)
    order = jnp.arange(count, dtype=jnp.int32)
    between = (order[:, None] < order[None, :]) & (order[None, :] < mine)
    exponent = jnp.sum(jnp.where(between[:, :, None], totals[None, :, :], 0.0), axis=1)
    weight = jnp.where((order < mine)[:, None], jnp.exp(exponent), 0.0)
    return jnp.sum(weight[:, :, None, None] * finals, axis=0)


def shards(frames, log_decay, w_query, w_key, w_value, w_gate, w_out):
    head_width = w_query.shape[1]
    blocks = [w_query, w_key, w_value, w_gate, w_out]
    width = sum(block.shape[1] for block in blocks)
    packed = sum(
        jnp.pad(block, ((0, 0), (start, width - start - block.shape[1])))
        for start, block in zip(range(0, width, head_width), blocks)
    )
    stacked = lax.all_gather(packed, "tm", axis=0, tiled=True)
    joined = stacked[:, : 4 * head_width]
    out_blocks = stacked[:, 4 * head_width :].reshape(-1, head_width, w_out.shape[1])
    frames_here = gather_by_exchange(frames, "head").reshape(-1, frames.shape[1])
    projected = jnp.dot(
        frames_here,
        joined,
        preferred_element_type=jnp.float32,
    )
    local_len = projected.shape[0]
    heads_here = head_width // HEAD_DIM
    block_count = local_len // BLOCK
    query_blocks = (
        projected[:, :head_width]
        .astype(jnp.bfloat16)
        .reshape(block_count, BLOCK, heads_here, HEAD_DIM)
    )
    key_blocks = (
        projected[:, head_width : 2 * head_width]
        .astype(jnp.bfloat16)
        .reshape(block_count, BLOCK, heads_here, HEAD_DIM)
    )
    value_blocks = (
        projected[:, 2 * head_width : 3 * head_width]
        .astype(jnp.bfloat16)
        .reshape(block_count, BLOCK, heads_here, HEAD_DIM)
    )
    gate_all = projected[:, 3 * head_width :]
    running_blocks = jnp.cumsum(log_decay.reshape(block_count, BLOCK, heads_here), axis=1)
    slice_ordinal = jnp.arange(BLOCK, dtype=jnp.int32)
    causal = slice_ordinal[:, None] >= slice_ordinal[None, :]

    def local_step(carry_state, inputs):
        query_block, key_block, value_block, running = inputs
        gaps = running.T[:, :, None] - running.T[:, None, :]
        decay = jnp.exp(jnp.where(causal[None], gaps, -jnp.inf))
        scores = jnp.einsum(
            "thd,shd->hts", query_block, key_block, preferred_element_type=jnp.float32
        )
        weights = (scores * decay).astype(jnp.bfloat16)
        intra = jnp.einsum("hts,shd->thd", weights, value_block, preferred_element_type=jnp.float32)
        scaled = (
            key_block.astype(jnp.float32) * jnp.exp(running[-1][None, :] - running)[:, :, None]
        ).astype(jnp.bfloat16)
        update = jnp.einsum("shd,she->hde", scaled, value_block, preferred_element_type=jnp.float32)
        next_state = jnp.exp(running[-1])[:, None, None] * carry_state + update
        return (next_state, (intra, carry_state))

    zero_state = jnp.zeros((heads_here, HEAD_DIM, HEAD_DIM), jnp.float32)
    local_final, (intra_all, local_starts) = lax.scan(
        local_step, zero_state, (query_blocks, key_blocks, value_blocks, running_blocks)
    )
    prior = prior_state(local_final, jnp.sum(log_decay, axis=0), "tm")
    block_logs = running_blocks[:, -1, :]
    before = jnp.cumsum(block_logs, axis=0) - block_logs
    start_states = jnp.exp(before)[:, :, None, None] * prior[None] + local_starts
    lifted = query_blocks.astype(jnp.float32) * jnp.exp(running_blocks)[..., None]
    inter = jnp.einsum("cthd,chde->cthe", lifted, start_states, precision=lax.Precision.HIGHEST)
    retained = (intra_all + inter).reshape(local_len, heads_here, HEAD_DIM)
    center = jnp.mean(retained, axis=-1, keepdims=True)
    spread = jnp.mean((retained - center) ** 2, axis=-1, keepdims=True)
    normed = (retained - center) / jnp.sqrt(spread + 1e-05)
    gated = (
        (jax.nn.silu(gate_all.reshape(local_len, heads_here, HEAD_DIM)) * normed)
        .astype(jnp.bfloat16)
        .reshape(local_len, head_width)
    )
    heads = lax.axis_size("head")
    side = int(round(heads ** 0.5))
    me = lax.axis_index("head")
    row, col = me // side, me % side
    rows_mine = out_blocks
    by_owner = gated.reshape(side, side, local_len // heads, head_width)
    units = lax.axis_size("tm")
    half = rows_mine.shape[0] // 2
    parity = lax.axis_index("tm") % 2
    own_half = lax.dynamic_slice_in_dim(rows_mine, parity * half, half, axis=0)
    fetched = []
    for shift in range(1, side):
        across = [(h, (h // side) * side + (h % side + shift) % side) for h in range(heads)]
        fetched.append(lax.ppermute(own_half, "head", across))
    fetched = jnp.stack(fetched)
    swapped = lax.ppermute(fetched, "tm", [(t, t ^ 1) for t in range(units)])
    first = jnp.where(parity == 0, fetched, swapped)
    second = jnp.where(parity == 0, swapped, fetched)
    remote = jnp.concatenate([first, second], axis=1)
    by_shift = jnp.concatenate([rows_mine[None], remote], axis=0)
    weights_in = jnp.take(by_shift, (col - jnp.arange(side)) % side, axis=0)
    across_ring = [[r * side + c for c in range(side)] for r in range(side)]
    down_ring = [[r * side + c for r in range(side)] for c in range(side)]
    pieces = lax.all_to_all(
        jnp.swapaxes(by_owner, 0, 1), "head", 0, 0, tiled=False, axis_index_groups=across_ring
    )
    partial = jnp.einsum(
        "syfr,skrc->yfkc",
        pieces,
        weights_in,
        preferred_element_type=jnp.float32,
    ).astype(jnp.bfloat16)
    partial = partial.reshape(side, local_len // heads, -1)
    shares = lax.all_to_all(partial, "head", 0, 0, tiled=False, axis_index_groups=down_ring)
    total = jnp.sum(shares.astype(jnp.float32), axis=0)
    return total.astype(jnp.bfloat16)


def solution(mesh):
    return jax.shard_map(
        shards,
        mesh=mesh,
        in_specs=(
            P(("tm", "head"), None),
            P("tm", "head"),
            P("tm", "head"),
            P("tm", "head"),
            P("tm", "head"),
            P("tm", "head"),
            P("head", "tm"),
        ),
        out_specs=P(("tm", "head"), None),
        check_vma=False,
    )
```

```python
import jax
import jax.numpy as jnp
from jax import lax
from jax.sharding import PartitionSpec as P

HEAD_DIM = 128
BLOCK = 512
PAD_ROWS = 8


def gather_by_exchange(part, axis):
    count = lax.axis_size(axis)
    copies = jnp.broadcast_to(part[None], (count,) + part.shape)
    return lax.all_to_all(copies, axis, 0, 0, tiled=False)


def prior_state(local_final, log_total, axis):
    heads_here = local_final.shape[0]
    high = log_total.astype(jnp.bfloat16)
    low = (log_total - high.astype(jnp.float32)).astype(jnp.bfloat16)
    extra = jnp.concatenate(
        [
            jnp.broadcast_to(high[:, None, None], (heads_here, 1, HEAD_DIM)),
            jnp.broadcast_to(low[:, None, None], (heads_here, 1, HEAD_DIM)),
            jnp.zeros((heads_here, PAD_ROWS - 2, HEAD_DIM), jnp.bfloat16),
        ],
        axis=1,
    )
    packed = jnp.concatenate([local_final.astype(jnp.bfloat16), extra], axis=1)
    gathered = gather_by_exchange(packed, axis)
    finals = gathered[:, :, :HEAD_DIM, :].astype(jnp.float32)
    totals = gathered[:, :, HEAD_DIM, 0].astype(jnp.float32) + gathered[:, :, HEAD_DIM + 1, 0].astype(
        jnp.float32
    )
    count = gathered.shape[0]
    mine = lax.axis_index(axis)
    order = jnp.arange(count, dtype=jnp.int32)
    between = (order[:, None] < order[None, :]) & (order[None, :] < mine)
    exponent = jnp.sum(jnp.where(between[:, :, None], totals[None, :, :], 0.0), axis=1)
    weight = jnp.where((order < mine)[:, None], jnp.exp(exponent), 0.0)
    return jnp.sum(weight[:, :, None, None] * finals, axis=0)


def shards(frames, log_decay, w_query, w_key, w_value, w_gate, w_out):
    head_width = w_query.shape[1]
    blocks = [w_query, w_key, w_value, w_gate, w_out]
    width = sum(block.shape[1] for block in blocks)
    packed = sum(
        jnp.pad(block, ((0, 0), (start, width - start - block.shape[1])))
        for start, block in zip(range(0, width, head_width), blocks)
    )
    stacked = lax.all_gather(packed, "tm", axis=0, tiled=True)
    joined = stacked[:, : 4 * head_width]
    out_blocks = stacked[:, 4 * head_width :].reshape(-1, head_width, w_out.shape[1])
    frames_here = gather_by_exchange(frames, "head").reshape(-1, frames.shape[1])
    projected = jnp.dot(
        frames_here,
        joined,
        preferred_element_type=jnp.float32,
    )
    local_len = projected.shape[0]
    heads_here = head_width // HEAD_DIM
    block_count = local_len // BLOCK
    query_blocks = (
        projected[:, :head_width]
        .astype(jnp.bfloat16)
        .reshape(block_count, BLOCK, heads_here, HEAD_DIM)
    )
    key_blocks = (
        projected[:, head_width : 2 * head_width]
        .astype(jnp.bfloat16)
        .reshape(block_count, BLOCK, heads_here, HEAD_DIM)
    )
    value_blocks = (
        projected[:, 2 * head_width : 3 * head_width]
        .astype(jnp.bfloat16)
        .reshape(block_count, BLOCK, heads_here, HEAD_DIM)
    )
    gate_all = projected[:, 3 * head_width :]
    running_blocks = jnp.cumsum(log_decay.reshape(block_count, BLOCK, heads_here), axis=1)
    slice_ordinal = jnp.arange(BLOCK, dtype=jnp.int32)
    causal = slice_ordinal[:, None] >= slice_ordinal[None, :]

    def local_step(carry_state, inputs):
        query_block, key_block, value_block, running = inputs
        gaps = running.T[:, :, None] - running.T[:, None, :]
        decay = jnp.exp(jnp.where(causal[None], gaps, -jnp.inf))
        scores = jnp.einsum(
            "thd,shd->hts", query_block, key_block, preferred_element_type=jnp.float32
        )
        weights = (scores * decay).astype(jnp.bfloat16)
        intra = jnp.einsum("hts,shd->thd", weights, value_block, preferred_element_type=jnp.float32)
        scaled = (
            key_block.astype(jnp.float32) * jnp.exp(running[-1][None, :] - running)[:, :, None]
        ).astype(jnp.bfloat16)
        update = jnp.einsum("shd,she->hde", scaled, value_block, preferred_element_type=jnp.float32)
        next_state = jnp.exp(running[-1])[:, None, None] * carry_state + update
        return (next_state, (intra, carry_state))

    zero_state = jnp.zeros((heads_here, HEAD_DIM, HEAD_DIM), jnp.float32)
    local_final, (intra_all, local_starts) = lax.scan(
        local_step, zero_state, (query_blocks, key_blocks, value_blocks, running_blocks)
    )
    prior = prior_state(local_final, jnp.sum(log_decay, axis=0), "tm")
    block_logs = running_blocks[:, -1, :]
    before = jnp.cumsum(block_logs, axis=0) - block_logs
    start_states = jnp.exp(before)[:, :, None, None] * prior[None] + local_starts
    lifted = query_blocks.astype(jnp.float32) * jnp.exp(running_blocks)[..., None]
    inter = jnp.einsum("cthd,chde->cthe", lifted, start_states, precision=lax.Precision.HIGHEST)
    retained = (intra_all + inter).reshape(local_len, heads_here, HEAD_DIM)
    center = jnp.mean(retained, axis=-1, keepdims=True)
    spread = jnp.mean((retained - center) ** 2, axis=-1, keepdims=True)
    normed = (retained - center) / jnp.sqrt(spread + 1e-05)
    gated = (
        (jax.nn.silu(gate_all.reshape(local_len, heads_here, HEAD_DIM)) * normed)
        .astype(jnp.bfloat16)
        .reshape(local_len, head_width)
    )
    heads = lax.axis_size("head")
    side = int(round(heads ** 0.5))
    me = lax.axis_index("head")
    row, col = me // side, me % side
    rows_mine = out_blocks
    ring_order = sorted(range(1, side), key=lambda shift: -min(shift, side - shift))
    by_owner = gated.reshape(side, side, local_len // heads, head_width)
    units = lax.axis_size("tm")
    half = rows_mine.shape[0] // 2
    parity = lax.axis_index("tm") % 2
    own_half = lax.dynamic_slice_in_dim(rows_mine, parity * half, half, axis=0)
    pieces = [lax.dynamic_index_in_dim(by_owner, col, axis=1, keepdims=False)]
    fetched = []
    for shift in ring_order:
        across = [(h, (h // side) * side + (h % side + shift) % side) for h in range(heads)]
        piece = lax.dynamic_index_in_dim(by_owner, (col + shift) % side, axis=1, keepdims=False)
        pieces.append(lax.ppermute(piece, "head", across))
        fetched.append(lax.ppermute(own_half, "head", across))
    fetched = jnp.stack(fetched)
    swapped = lax.ppermute(fetched, "tm", [(t, t ^ 1) for t in range(units)])
    first = jnp.where(parity == 0, fetched, swapped)
    second = jnp.where(parity == 0, swapped, fetched)
    remote = jnp.concatenate([first, second], axis=1)
    weights_in = [rows_mine] + [remote[s] for s in range(side - 1)]
    partial = jnp.einsum(
        "syfr,skrc->yfkc",
        jnp.stack(pieces),
        jnp.stack(weights_in),
        preferred_element_type=jnp.float32,
    ).astype(jnp.bfloat16)
    partial = partial.reshape(side, local_len // heads, -1)
    total = lax.dynamic_index_in_dim(partial, row, axis=0, keepdims=False).astype(jnp.float32)
    for shift in ring_order:
        down = [(h, ((h // side + shift) % side) * side + h % side) for h in range(heads)]
        piece = lax.dynamic_index_in_dim(partial, (row + shift) % side, axis=0, keepdims=False)
        total = total + lax.ppermute(piece, "head", down).astype(jnp.float32)
    return total.astype(jnp.bfloat16)


def solution(mesh):
    return jax.shard_map(
        shards,
        mesh=mesh,
        in_specs=(
            P(("tm", "head"), None),
            P("tm", "head"),
            P("tm", "head"),
            P("tm", "head"),
            P("tm", "head"),
            P("tm", "head"),
            P("head", "tm"),
        ),
        out_specs=P(("tm", "head"), None),
        check_vma=False,
    )
```

```python
import jax
import jax.numpy as jnp
from jax import lax
from jax.sharding import PartitionSpec as P

HEAD_DIM = 128
BLOCK = 512
PAD_ROWS = 8


def gather_by_exchange(part, axis):
    count = lax.axis_size(axis)
    copies = jnp.broadcast_to(part[None], (count,) + part.shape)
    return lax.all_to_all(copies, axis, 0, 0, tiled=False)


def prior_state(local_final, log_total, axis):
    heads_here = local_final.shape[0]
    high = log_total.astype(jnp.bfloat16)
    low = (log_total - high.astype(jnp.float32)).astype(jnp.bfloat16)
    extra = jnp.concatenate(
        [
            jnp.broadcast_to(high[:, None, None], (heads_here, 1, HEAD_DIM)),
            jnp.broadcast_to(low[:, None, None], (heads_here, 1, HEAD_DIM)),
            jnp.zeros((heads_here, PAD_ROWS - 2, HEAD_DIM), jnp.bfloat16),
        ],
        axis=1,
    )
    packed = jnp.concatenate([local_final.astype(jnp.bfloat16), extra], axis=1)
    gathered = gather_by_exchange(packed, axis)
    finals = gathered[:, :, :HEAD_DIM, :].astype(jnp.float32)
    totals = gathered[:, :, HEAD_DIM, 0].astype(jnp.float32) + gathered[:, :, HEAD_DIM + 1, 0].astype(
        jnp.float32
    )
    count = gathered.shape[0]
    mine = lax.axis_index(axis)
    order = jnp.arange(count, dtype=jnp.int32)
    between = (order[:, None] < order[None, :]) & (order[None, :] < mine)
    exponent = jnp.sum(jnp.where(between[:, :, None], totals[None, :, :], 0.0), axis=1)
    weight = jnp.where((order < mine)[:, None], jnp.exp(exponent), 0.0)
    return jnp.sum(weight[:, :, None, None] * finals, axis=0)


def shards(frames, log_decay, w_query, w_key, w_value, w_gate, w_out):
    head_width = w_query.shape[1]
    blocks = [w_query, w_key, w_value, w_gate, w_out]
    width = sum(block.shape[1] for block in blocks)
    packed = sum(
        jnp.pad(block, ((0, 0), (start, width - start - block.shape[1])))
        for start, block in zip(range(0, width, head_width), blocks)
    )
    stacked = lax.all_gather(packed, "tm", axis=0, tiled=True)
    joined = stacked[:, : 4 * head_width]
    out_blocks = stacked[:, 4 * head_width :].reshape(-1, head_width, w_out.shape[1])
    frames_here = gather_by_exchange(frames, "head").reshape(-1, frames.shape[1])
    projected = jnp.dot(
        frames_here,
        joined,
        preferred_element_type=jnp.float32,
    )
    local_len = projected.shape[0]
    heads_here = head_width // HEAD_DIM
    block_count = local_len // BLOCK
    query_blocks = (
        projected[:, :head_width]
        .astype(jnp.bfloat16)
        .reshape(block_count, BLOCK, heads_here, HEAD_DIM)
    )
    key_blocks = (
        projected[:, head_width : 2 * head_width]
        .astype(jnp.bfloat16)
        .reshape(block_count, BLOCK, heads_here, HEAD_DIM)
    )
    value_blocks = (
        projected[:, 2 * head_width : 3 * head_width]
        .astype(jnp.bfloat16)
        .reshape(block_count, BLOCK, heads_here, HEAD_DIM)
    )
    gate_all = projected[:, 3 * head_width :]
    running_blocks = jnp.cumsum(log_decay.reshape(block_count, BLOCK, heads_here), axis=1)
    slice_ordinal = jnp.arange(BLOCK, dtype=jnp.int32)
    causal = slice_ordinal[:, None] >= slice_ordinal[None, :]

    def local_step(carry_state, inputs):
        query_block, key_block, value_block, running = inputs
        gaps = running.T[:, :, None] - running.T[:, None, :]
        decay = jnp.exp(jnp.where(causal[None], gaps, -jnp.inf))
        scores = jnp.einsum(
            "thd,shd->hts", query_block, key_block, preferred_element_type=jnp.float32
        )
        weights = (scores * decay).astype(jnp.bfloat16)
        intra = jnp.einsum("hts,shd->thd", weights, value_block, preferred_element_type=jnp.float32)
        scaled = (
            key_block.astype(jnp.float32) * jnp.exp(running[-1][None, :] - running)[:, :, None]
        ).astype(jnp.bfloat16)
        update = jnp.einsum("shd,she->hde", scaled, value_block, preferred_element_type=jnp.float32)
        next_state = jnp.exp(running[-1])[:, None, None] * carry_state + update
        return (next_state, (intra, carry_state))

    zero_state = jnp.zeros((heads_here, HEAD_DIM, HEAD_DIM), jnp.float32)
    local_final, (intra_all, local_starts) = lax.scan(
        local_step, zero_state, (query_blocks, key_blocks, value_blocks, running_blocks)
    )
    prior = prior_state(local_final, jnp.sum(log_decay, axis=0), "tm")
    block_logs = running_blocks[:, -1, :]
    before = jnp.cumsum(block_logs, axis=0) - block_logs
    start_states = jnp.exp(before)[:, :, None, None] * prior[None] + local_starts
    lifted = query_blocks.astype(jnp.float32) * jnp.exp(running_blocks)[..., None]
    inter = jnp.einsum("cthd,chde->cthe", lifted, start_states, precision=lax.Precision.HIGHEST)
    retained = (intra_all + inter).reshape(local_len, heads_here, HEAD_DIM)
    center = jnp.mean(retained, axis=-1, keepdims=True)
    spread = jnp.mean((retained - center) ** 2, axis=-1, keepdims=True)
    normed = (retained - center) / jnp.sqrt(spread + 1e-05)
    gated = (
        (jax.nn.silu(gate_all.reshape(local_len, heads_here, HEAD_DIM)) * normed)
        .astype(jnp.bfloat16)
        .reshape(local_len, head_width)
    )
    heads = lax.axis_size("head")
    side = int(round(heads ** 0.5))
    me = lax.axis_index("head")
    row, col = me // side, me % side
    rows_mine = out_blocks
    ring_order = sorted(range(1, side), key=lambda shift: -min(shift, side - shift))
    by_owner = gated.reshape(side, side, local_len // heads, head_width)
    units = lax.axis_size("tm")
    half = rows_mine.shape[0] // 2
    parity = lax.axis_index("tm") % 2
    own_half = lax.dynamic_slice_in_dim(rows_mine, parity * half, half, axis=0)
    pieces = [lax.dynamic_index_in_dim(by_owner, col, axis=1, keepdims=False)]
    fetched = []
    for shift in ring_order:
        across = [(h, (h // side) * side + (h % side + shift) % side) for h in range(heads)]
        piece = lax.dynamic_index_in_dim(by_owner, (col + shift) % side, axis=1, keepdims=False)
        pieces.append(lax.ppermute(piece, "head", across))
        fetched.append(lax.ppermute(own_half, "head", across))
    fetched = jnp.stack(fetched)
    swapped = lax.ppermute(fetched, "tm", [(t, t ^ 1) for t in range(units)])
    first = jnp.where(parity == 0, fetched, swapped)
    second = jnp.where(parity == 0, swapped, fetched)
    remote = jnp.concatenate([first, second], axis=1)
    weights_in = [rows_mine] + [remote[s] for s in range(side - 1)]
    gathered_pieces = jnp.stack(pieces)
    gathered_rows = jnp.stack(weights_in)

    def partial_for(destination):
        rows_for = lax.dynamic_index_in_dim(gathered_pieces, destination, axis=1, keepdims=False)
        return (
            jnp.einsum(
                "sfr,skrc->fkc", rows_for, gathered_rows, preferred_element_type=jnp.float32
            )
            .astype(jnp.bfloat16)
            .reshape(local_len // heads, -1)
        )

    received = []
    for shift in ring_order:
        down = [(h, ((h // side + shift) % side) * side + h % side) for h in range(heads)]
        received.append(lax.ppermute(partial_for((row + shift) % side), "head", down))
    total = partial_for(row).astype(jnp.float32)
    for piece in received:
        total = total + piece.astype(jnp.float32)
    return total.astype(jnp.bfloat16)


def solution(mesh):
    return jax.shard_map(
        shards,
        mesh=mesh,
        in_specs=(
            P(("tm", "head"), None),
            P("tm", "head"),
            P("tm", "head"),
            P("tm", "head"),
            P("tm", "head"),
            P("tm", "head"),
            P("head", "tm"),
        ),
        out_specs=P(("tm", "head"), None),
        check_vma=False,
    )
```

```python
import jax
import jax.numpy as jnp
from jax import lax
from jax.sharding import PartitionSpec as P

HEAD_DIM = 128
BLOCK = 512
PAD_ROWS = 8


def gather_by_exchange(part, axis):
    count = lax.axis_size(axis)
    copies = jnp.broadcast_to(part[None], (count,) + part.shape)
    return lax.all_to_all(copies, axis, 0, 0, tiled=False)


def prior_state(local_final, totals, axis):
    count = totals.shape[0]
    mine = lax.axis_index(axis)
    order = jnp.arange(count, dtype=jnp.int32)
    between = (order[:, None] < order[None, :]) & (order[None, :] < mine)
    exponent = jnp.sum(jnp.where(between[:, :, None], totals[None, :, :], 0.0), axis=1)
    weight = jnp.where((order < mine)[:, None], jnp.exp(exponent), 0.0)
    finals = gather_by_exchange(local_final.astype(jnp.bfloat16), axis).astype(jnp.float32)
    return jnp.sum(weight[:, :, None, None] * finals, axis=0)


def shards(frames, log_decay, w_query, w_key, w_value, w_gate, w_out):
    head_width = w_query.shape[1]
    log_total = jnp.sum(log_decay, axis=0)
    high = log_total.astype(jnp.bfloat16)
    low = (log_total - high.astype(jnp.float32)).astype(jnp.bfloat16)
    row_index = jnp.arange(w_query.shape[0])[:, None]
    totals_block = jnp.where(
        row_index == 0,
        jnp.repeat(high, HEAD_DIM)[None, :],
        jnp.where(row_index == 1, jnp.repeat(low, HEAD_DIM)[None, :], jnp.zeros((), jnp.bfloat16)),
    )
    blocks = [w_query, w_key, w_value, w_gate, w_out, totals_block]
    width = sum(block.shape[1] for block in blocks)
    packed = sum(
        jnp.pad(block, ((0, 0), (start, width - start - block.shape[1])))
        for start, block in zip(range(0, width, head_width), blocks)
    )
    stacked = lax.all_gather(packed, "tm", axis=0, tiled=True)
    joined = stacked[:, : 4 * head_width]
    out_blocks = stacked[:, 4 * head_width : 5 * head_width].reshape(-1, head_width, w_out.shape[1])
    totals_rows = stacked[:, 5 * head_width :].reshape(-1, w_query.shape[0], head_width // HEAD_DIM, HEAD_DIM)
    totals = totals_rows[:, 0, :, 0].astype(jnp.float32) + totals_rows[:, 1, :, 0].astype(jnp.float32)
    frames_here = gather_by_exchange(frames, "head").reshape(-1, frames.shape[1])
    projected = jnp.dot(
        frames_here,
        joined,
        preferred_element_type=jnp.float32,
    )
    local_len = projected.shape[0]
    heads_here = head_width // HEAD_DIM
    block_count = local_len // BLOCK
    query_blocks = (
        projected[:, :head_width]
        .astype(jnp.bfloat16)
        .reshape(block_count, BLOCK, heads_here, HEAD_DIM)
    )
    key_blocks = (
        projected[:, head_width : 2 * head_width]
        .astype(jnp.bfloat16)
        .reshape(block_count, BLOCK, heads_here, HEAD_DIM)
    )
    value_blocks = (
        projected[:, 2 * head_width : 3 * head_width]
        .astype(jnp.bfloat16)
        .reshape(block_count, BLOCK, heads_here, HEAD_DIM)
    )
    gate_all = projected[:, 3 * head_width :]
    running_blocks = jnp.cumsum(log_decay.reshape(block_count, BLOCK, heads_here), axis=1)
    slice_ordinal = jnp.arange(BLOCK, dtype=jnp.int32)
    causal = slice_ordinal[:, None] >= slice_ordinal[None, :]

    def local_step(carry_state, inputs):
        query_block, key_block, value_block, running = inputs
        gaps = running.T[:, :, None] - running.T[:, None, :]
        decay = jnp.exp(jnp.where(causal[None], gaps, -jnp.inf))
        scores = jnp.einsum(
            "thd,shd->hts", query_block, key_block, preferred_element_type=jnp.float32
        )
        weights = (scores * decay).astype(jnp.bfloat16)
        intra = jnp.einsum("hts,shd->thd", weights, value_block, preferred_element_type=jnp.float32)
        scaled = (
            key_block.astype(jnp.float32) * jnp.exp(running[-1][None, :] - running)[:, :, None]
        ).astype(jnp.bfloat16)
        update = jnp.einsum("shd,she->hde", scaled, value_block, preferred_element_type=jnp.float32)
        next_state = jnp.exp(running[-1])[:, None, None] * carry_state + update
        return (next_state, (intra, carry_state))

    zero_state = jnp.zeros((heads_here, HEAD_DIM, HEAD_DIM), jnp.float32)
    local_final, (intra_all, local_starts) = lax.scan(
        local_step, zero_state, (query_blocks, key_blocks, value_blocks, running_blocks)
    )
    prior = prior_state(local_final, totals, "tm")
    block_logs = running_blocks[:, -1, :]
    before = jnp.cumsum(block_logs, axis=0) - block_logs
    start_states = jnp.exp(before)[:, :, None, None] * prior[None] + local_starts
    lifted = query_blocks.astype(jnp.float32) * jnp.exp(running_blocks)[..., None]
    inter = jnp.einsum("cthd,chde->cthe", lifted, start_states, precision=lax.Precision.HIGHEST)
    retained = (intra_all + inter).reshape(local_len, heads_here, HEAD_DIM)
    center = jnp.mean(retained, axis=-1, keepdims=True)
    spread = jnp.mean((retained - center) ** 2, axis=-1, keepdims=True)
    normed = (retained - center) / jnp.sqrt(spread + 1e-05)
    gated = (
        (jax.nn.silu(gate_all.reshape(local_len, heads_here, HEAD_DIM)) * normed)
        .astype(jnp.bfloat16)
        .reshape(local_len, head_width)
    )
    heads = lax.axis_size("head")
    side = int(round(heads ** 0.5))
    me = lax.axis_index("head")
    row, col = me // side, me % side
    rows_mine = out_blocks
    ring_order = sorted(range(1, side), key=lambda shift: -min(shift, side - shift))
    by_owner = gated.reshape(side, side, local_len // heads, head_width)
    units = lax.axis_size("tm")
    half = rows_mine.shape[0] // 2
    parity = lax.axis_index("tm") % 2
    own_half = lax.dynamic_slice_in_dim(rows_mine, parity * half, half, axis=0)
    pieces = [lax.dynamic_index_in_dim(by_owner, col, axis=1, keepdims=False)]
    fetched = []
    for shift in ring_order:
        across = [(h, (h // side) * side + (h % side + shift) % side) for h in range(heads)]
        piece = lax.dynamic_index_in_dim(by_owner, (col + shift) % side, axis=1, keepdims=False)
        pieces.append(lax.ppermute(piece, "head", across))
        fetched.append(lax.ppermute(own_half, "head", across))
    fetched = jnp.stack(fetched)
    swapped = lax.ppermute(fetched, "tm", [(t, t ^ 1) for t in range(units)])
    first = jnp.where(parity == 0, fetched, swapped)
    second = jnp.where(parity == 0, swapped, fetched)
    remote = jnp.concatenate([first, second], axis=1)
    weights_in = [rows_mine] + [remote[s] for s in range(side - 1)]
    partial = jnp.einsum(
        "syfr,skrc->yfkc",
        jnp.stack(pieces),
        jnp.stack(weights_in),
        preferred_element_type=jnp.float32,
    ).astype(jnp.bfloat16)
    partial = partial.reshape(side, local_len // heads, -1)
    total = lax.dynamic_index_in_dim(partial, row, axis=0, keepdims=False).astype(jnp.float32)
    for shift in ring_order:
        down = [(h, ((h // side + shift) % side) * side + h % side) for h in range(heads)]
        piece = lax.dynamic_index_in_dim(partial, (row + shift) % side, axis=0, keepdims=False)
        total = total + lax.ppermute(piece, "head", down).astype(jnp.float32)
    return total.astype(jnp.bfloat16)


def solution(mesh):
    return jax.shard_map(
        shards,
        mesh=mesh,
        in_specs=(
            P(("tm", "head"), None),
            P("tm", "head"),
            P("tm", "head"),
            P("tm", "head"),
            P("tm", "head"),
            P("tm", "head"),
            P("head", "tm"),
        ),
        out_specs=P(("tm", "head"), None),
        check_vma=False,
    )
```

```python
import jax
import jax.numpy as jnp
from jax import lax
from jax.sharding import PartitionSpec as P

HEAD_DIM = 128
BLOCK = 512
PAD_ROWS = 8


def gather_by_exchange(part, axis):
    count = lax.axis_size(axis)
    copies = jnp.broadcast_to(part[None], (count,) + part.shape)
    return lax.all_to_all(copies, axis, 0, 0, tiled=False)


def prior_state(local_final, log_total, axis):
    heads_here = local_final.shape[0]
    high = log_total.astype(jnp.bfloat16)
    low = (log_total - high.astype(jnp.float32)).astype(jnp.bfloat16)
    extra = jnp.concatenate(
        [
            jnp.broadcast_to(high[:, None, None], (heads_here, 1, HEAD_DIM)),
            jnp.broadcast_to(low[:, None, None], (heads_here, 1, HEAD_DIM)),
            jnp.zeros((heads_here, PAD_ROWS - 2, HEAD_DIM), jnp.bfloat16),
        ],
        axis=1,
    )
    packed = jnp.concatenate([local_final.astype(jnp.bfloat16), extra], axis=1)
    gathered = gather_by_exchange(packed, axis)
    finals = gathered[:, :, :HEAD_DIM, :].astype(jnp.float32)
    totals = gathered[:, :, HEAD_DIM, 0].astype(jnp.float32) + gathered[:, :, HEAD_DIM + 1, 0].astype(
        jnp.float32
    )
    count = gathered.shape[0]
    mine = lax.axis_index(axis)
    order = jnp.arange(count, dtype=jnp.int32)
    between = (order[:, None] < order[None, :]) & (order[None, :] < mine)
    exponent = jnp.sum(jnp.where(between[:, :, None], totals[None, :, :], 0.0), axis=1)
    weight = jnp.where((order < mine)[:, None], jnp.exp(exponent), 0.0)
    return jnp.sum(weight[:, :, None, None] * finals, axis=0)


def shards(frames, log_decay, w_query, w_key, w_value, w_gate, w_out):
    head_width = w_query.shape[1]
    blocks = [w_query, w_key, w_value, w_gate, w_out]
    width = sum(block.shape[1] for block in blocks)
    packed = sum(
        jnp.pad(block, ((0, 0), (start, width - start - block.shape[1])))
        for start, block in zip(range(0, width, head_width), blocks)
    )
    stacked = lax.all_gather(packed, "tm", axis=0, tiled=True)
    joined = stacked[:, : 4 * head_width]
    out_blocks = stacked[:, 4 * head_width :].reshape(-1, head_width, w_out.shape[1])
    frames_here = gather_by_exchange(frames, "head").reshape(-1, frames.shape[1])
    projected = jnp.dot(
        frames_here,
        joined,
        preferred_element_type=jnp.float32,
    )
    local_len = projected.shape[0]
    heads_here = head_width // HEAD_DIM
    block_count = local_len // BLOCK
    query_blocks = (
        projected[:, :head_width]
        .astype(jnp.bfloat16)
        .reshape(block_count, BLOCK, heads_here, HEAD_DIM)
    )
    key_blocks = (
        projected[:, head_width : 2 * head_width]
        .astype(jnp.bfloat16)
        .reshape(block_count, BLOCK, heads_here, HEAD_DIM)
    )
    value_blocks = (
        projected[:, 2 * head_width : 3 * head_width]
        .astype(jnp.bfloat16)
        .reshape(block_count, BLOCK, heads_here, HEAD_DIM)
    )
    gate_all = projected[:, 3 * head_width :]
    running_blocks = jnp.cumsum(log_decay.reshape(block_count, BLOCK, heads_here), axis=1)
    slice_ordinal = jnp.arange(BLOCK, dtype=jnp.int32)
    causal = slice_ordinal[:, None] >= slice_ordinal[None, :]

    def local_step(carry_state, inputs):
        query_block, key_block, value_block, running = inputs
        gaps = running.T[:, :, None] - running.T[:, None, :]
        decay = jnp.exp(jnp.where(causal[None], gaps, -jnp.inf))
        scores = jnp.einsum(
            "thd,shd->hts", query_block, key_block, preferred_element_type=jnp.float32
        )
        weights = (scores * decay).astype(jnp.bfloat16)
        intra = jnp.einsum("hts,shd->thd", weights, value_block, preferred_element_type=jnp.float32)
        scaled = (
            key_block.astype(jnp.float32) * jnp.exp(running[-1][None, :] - running)[:, :, None]
        ).astype(jnp.bfloat16)
        update = jnp.einsum("shd,she->hde", scaled, value_block, preferred_element_type=jnp.float32)
        next_state = jnp.exp(running[-1])[:, None, None] * carry_state + update
        return (next_state, (intra, carry_state))

    zero_state = jnp.zeros((heads_here, HEAD_DIM, HEAD_DIM), jnp.float32)
    local_final, (intra_all, local_starts) = lax.scan(
        local_step, zero_state, (query_blocks, key_blocks, value_blocks, running_blocks)
    )
    prior = prior_state(local_final, jnp.sum(log_decay, axis=0), "tm")
    block_logs = running_blocks[:, -1, :]
    before = jnp.cumsum(block_logs, axis=0) - block_logs
    start_states = jnp.exp(before)[:, :, None, None] * prior[None] + local_starts
    lifted = query_blocks.astype(jnp.float32) * jnp.exp(running_blocks)[..., None]
    inter = jnp.einsum(
        "cthd,chde->cthe",
        lifted.astype(jnp.bfloat16),
        start_states.astype(jnp.bfloat16),
        preferred_element_type=jnp.float32,
    )
    retained = (intra_all + inter).reshape(local_len, heads_here, HEAD_DIM)
    center = jnp.mean(retained, axis=-1, keepdims=True)
    spread = jnp.mean((retained - center) ** 2, axis=-1, keepdims=True)
    normed = (retained - center) * lax.rsqrt(spread + 1e-05)
    gated = (
        (jax.nn.silu(gate_all.reshape(local_len, heads_here, HEAD_DIM)) * normed)
        .astype(jnp.bfloat16)
        .reshape(local_len, head_width)
    )
    heads = lax.axis_size("head")
    side = int(round(heads ** 0.5))
    me = lax.axis_index("head")
    row, col = me // side, me % side
    rows_mine = out_blocks
    ring_order = sorted(range(1, side), key=lambda shift: -min(shift, side - shift))
    by_owner = gated.reshape(side, side, local_len // heads, head_width)
    units = lax.axis_size("tm")
    half = rows_mine.shape[0] // 2
    parity = lax.axis_index("tm") % 2
    own_half = lax.dynamic_slice_in_dim(rows_mine, parity * half, half, axis=0)
    pieces = [lax.dynamic_index_in_dim(by_owner, col, axis=1, keepdims=False)]
    fetched = []
    for shift in ring_order:
        across = [(h, (h // side) * side + (h % side + shift) % side) for h in range(heads)]
        piece = lax.dynamic_index_in_dim(by_owner, (col + shift) % side, axis=1, keepdims=False)
        pieces.append(lax.ppermute(piece, "head", across))
        fetched.append(lax.ppermute(own_half, "head", across))
    fetched = jnp.stack(fetched)
    swapped = lax.ppermute(fetched, "tm", [(t, t ^ 1) for t in range(units)])
    first = jnp.where(parity == 0, fetched, swapped)
    second = jnp.where(parity == 0, swapped, fetched)
    remote = jnp.concatenate([first, second], axis=1)
    weights_in = [rows_mine] + [remote[s] for s in range(side - 1)]
    partial = jnp.einsum(
        "syfr,skrc->yfkc",
        jnp.stack(pieces),
        jnp.stack(weights_in),
        preferred_element_type=jnp.float32,
    ).astype(jnp.bfloat16)
    partial = partial.reshape(side, local_len // heads, -1)
    total = lax.dynamic_index_in_dim(partial, row, axis=0, keepdims=False).astype(jnp.float32)
    for shift in ring_order:
        down = [(h, ((h // side + shift) % side) * side + h % side) for h in range(heads)]
        piece = lax.dynamic_index_in_dim(partial, (row + shift) % side, axis=0, keepdims=False)
        total = total + lax.ppermute(piece, "head", down).astype(jnp.float32)
    return total.astype(jnp.bfloat16)


def solution(mesh):
    return jax.shard_map(
        shards,
        mesh=mesh,
        in_specs=(
            P(("tm", "head"), None),
            P("tm", "head"),
            P("tm", "head"),
            P("tm", "head"),
            P("tm", "head"),
            P("tm", "head"),
            P("head", "tm"),
        ),
        out_specs=P(("tm", "head"), None),
        check_vma=False,
    )
```

```python
import jax
import jax.numpy as jnp
from jax import lax
from jax.sharding import PartitionSpec as P

HEAD_DIM = 128
BLOCK = 512
PAD_ROWS = 8


def gather_by_exchange(part, axis):
    count = lax.axis_size(axis)
    copies = jnp.broadcast_to(part[None], (count,) + part.shape)
    return lax.all_to_all(copies, axis, 0, 0, tiled=False)


def prior_state(local_final, log_total, axis):
    heads_here = local_final.shape[0]
    high = log_total.astype(jnp.bfloat16)
    low = (log_total - high.astype(jnp.float32)).astype(jnp.bfloat16)
    extra = jnp.concatenate(
        [
            jnp.broadcast_to(high[:, None, None], (heads_here, 1, HEAD_DIM)),
            jnp.broadcast_to(low[:, None, None], (heads_here, 1, HEAD_DIM)),
            jnp.zeros((heads_here, PAD_ROWS - 2, HEAD_DIM), jnp.bfloat16),
        ],
        axis=1,
    )
    packed = jnp.concatenate([local_final.astype(jnp.bfloat16), extra], axis=1)
    gathered = gather_by_exchange(packed, axis)
    finals = gathered[:, :, :HEAD_DIM, :].astype(jnp.float32)
    totals = gathered[:, :, HEAD_DIM, 0].astype(jnp.float32) + gathered[:, :, HEAD_DIM + 1, 0].astype(
        jnp.float32
    )
    count = gathered.shape[0]
    mine = lax.axis_index(axis)
    order = jnp.arange(count, dtype=jnp.int32)
    between = (order[:, None] < order[None, :]) & (order[None, :] < mine)
    exponent = jnp.sum(jnp.where(between[:, :, None], totals[None, :, :], 0.0), axis=1)
    weight = jnp.where((order < mine)[:, None], jnp.exp(exponent), 0.0)
    return jnp.sum(weight[:, :, None, None] * finals, axis=0)


def shards(frames, log_decay, w_query, w_key, w_value, w_gate, w_out):
    head_width = w_query.shape[1]
    blocks = [w_query, w_key, w_value, w_gate, w_out]
    width = sum(block.shape[1] for block in blocks)
    column = jnp.arange(width)[None, :]
    packed = jnp.pad(blocks[-1], ((0, 0), (width - head_width, 0)))
    for start, block in reversed(list(zip(range(0, width, head_width), blocks))[:-1]):
        padded = jnp.pad(block, ((0, 0), (start, width - start - head_width)))
        packed = jnp.where(column < start + head_width, padded, packed)
    stacked = lax.all_gather(packed, "tm", axis=0, tiled=True)
    joined = stacked[:, : 4 * head_width]
    out_blocks = stacked[:, 4 * head_width :].reshape(-1, head_width, w_out.shape[1])
    frames_here = gather_by_exchange(frames, "head").reshape(-1, frames.shape[1])
    projected = jnp.dot(
        frames_here,
        joined,
        preferred_element_type=jnp.float32,
    )
    local_len = projected.shape[0]
    heads_here = head_width // HEAD_DIM
    block_count = local_len // BLOCK
    query_blocks = (
        projected[:, :head_width]
        .astype(jnp.bfloat16)
        .reshape(block_count, BLOCK, heads_here, HEAD_DIM)
    )
    key_blocks = (
        projected[:, head_width : 2 * head_width]
        .astype(jnp.bfloat16)
        .reshape(block_count, BLOCK, heads_here, HEAD_DIM)
    )
    value_blocks = (
        projected[:, 2 * head_width : 3 * head_width]
        .astype(jnp.bfloat16)
        .reshape(block_count, BLOCK, heads_here, HEAD_DIM)
    )
    gate_all = projected[:, 3 * head_width :]
    running_blocks = jnp.cumsum(log_decay.reshape(block_count, BLOCK, heads_here), axis=1)
    slice_ordinal = jnp.arange(BLOCK, dtype=jnp.int32)
    causal = slice_ordinal[:, None] >= slice_ordinal[None, :]

    def local_step(carry_state, inputs):
        query_block, key_block, value_block, running = inputs
        gaps = running.T[:, :, None] - running.T[:, None, :]
        decay = jnp.exp(jnp.where(causal[None], gaps, -jnp.inf))
        scores = jnp.einsum(
            "thd,shd->hts", query_block, key_block, preferred_element_type=jnp.float32
        )
        weights = (scores * decay).astype(jnp.bfloat16)
        intra = jnp.einsum("hts,shd->thd", weights, value_block, preferred_element_type=jnp.float32)
        scaled = (
            key_block.astype(jnp.float32) * jnp.exp(running[-1][None, :] - running)[:, :, None]
        ).astype(jnp.bfloat16)
        update = jnp.einsum("shd,she->hde", scaled, value_block, preferred_element_type=jnp.float32)
        next_state = jnp.exp(running[-1])[:, None, None] * carry_state + update
        return (next_state, (intra, carry_state))

    zero_state = jnp.zeros((heads_here, HEAD_DIM, HEAD_DIM), jnp.float32)
    local_final, (intra_all, local_starts) = lax.scan(
        local_step, zero_state, (query_blocks, key_blocks, value_blocks, running_blocks)
    )
    prior = prior_state(local_final, jnp.sum(log_decay, axis=0), "tm")
    block_logs = running_blocks[:, -1, :]
    before = jnp.cumsum(block_logs, axis=0) - block_logs
    start_states = jnp.exp(before)[:, :, None, None] * prior[None] + local_starts
    lifted = query_blocks.astype(jnp.float32) * jnp.exp(running_blocks)[..., None]
    inter = jnp.einsum("cthd,chde->cthe", lifted, start_states, precision=lax.Precision.HIGHEST)
    retained = (intra_all + inter).reshape(local_len, heads_here, HEAD_DIM)
    center = jnp.mean(retained, axis=-1, keepdims=True)
    spread = jnp.mean((retained - center) ** 2, axis=-1, keepdims=True)
    normed = (retained - center) / jnp.sqrt(spread + 1e-05)
    gated = (
        (jax.nn.silu(gate_all.reshape(local_len, heads_here, HEAD_DIM)) * normed)
        .astype(jnp.bfloat16)
        .reshape(local_len, head_width)
    )
    heads = lax.axis_size("head")
    side = int(round(heads ** 0.5))
    me = lax.axis_index("head")
    row, col = me // side, me % side
    rows_mine = out_blocks
    ring_order = sorted(range(1, side), key=lambda shift: -min(shift, side - shift))
    by_owner = gated.reshape(side, side, local_len // heads, head_width)
    units = lax.axis_size("tm")
    half = rows_mine.shape[0] // 2
    parity = lax.axis_index("tm") % 2
    own_half = lax.dynamic_slice_in_dim(rows_mine, parity * half, half, axis=0)
    pieces = [lax.dynamic_index_in_dim(by_owner, col, axis=1, keepdims=False)]
    fetched = []
    for shift in ring_order:
        across = [(h, (h // side) * side + (h % side + shift) % side) for h in range(heads)]
        piece = lax.dynamic_index_in_dim(by_owner, (col + shift) % side, axis=1, keepdims=False)
        pieces.append(lax.ppermute(piece, "head", across))
        fetched.append(lax.ppermute(own_half, "head", across))
    fetched = jnp.stack(fetched)
    swapped = lax.ppermute(fetched, "tm", [(t, t ^ 1) for t in range(units)])
    first = jnp.where(parity == 0, fetched, swapped)
    second = jnp.where(parity == 0, swapped, fetched)
    remote = jnp.concatenate([first, second], axis=1)
    weights_in = [rows_mine] + [remote[s] for s in range(side - 1)]
    partial = jnp.einsum(
        "syfr,skrc->yfkc",
        jnp.stack(pieces),
        jnp.stack(weights_in),
        preferred_element_type=jnp.float32,
    ).astype(jnp.bfloat16)
    partial = partial.reshape(side, local_len // heads, -1)
    total = lax.dynamic_index_in_dim(partial, row, axis=0, keepdims=False).astype(jnp.float32)
    for shift in ring_order:
        down = [(h, ((h // side + shift) % side) * side + h % side) for h in range(heads)]
        piece = lax.dynamic_index_in_dim(partial, (row + shift) % side, axis=0, keepdims=False)
        total = total + lax.ppermute(piece, "head", down).astype(jnp.float32)
    return total.astype(jnp.bfloat16)


def solution(mesh):
    return jax.shard_map(
        shards,
        mesh=mesh,
        in_specs=(
            P(("tm", "head"), None),
            P("tm", "head"),
            P("tm", "head"),
            P("tm", "head"),
            P("tm", "head"),
            P("tm", "head"),
            P("head", "tm"),
        ),
        out_specs=P(("tm", "head"), None),
        check_vma=False,
    )
```
